256 devices in a mesh: rad: 8 (over y, z_lo), az: 32 (over x, z_hi, core).
Axes of the slice: x: 4, y: 4, z: 8 (z_hi: 4, z_lo: 2; z = z_hi * 2 + z_lo), core: 2. Of those that a mesh axis runs over, the one named last changes fastest.
Arguments:
- dust_density: float32 [512, 512, 128], P('rad', 'az'), may hold values from 0.05 to 1
- dust_velocity: float32 [512, 512, 2, 128], P('rad', 'az'), may hold values from -6 to 6
- gas_density: float32 [1024, 2048], P('rad', 'az'), may hold values from 0.5 to 2
- gas_velocity: float32 [1024, 2, 2048], P('rad', None, 'az'), may hold values from -6 to 6
- kernel: float32 [128, 128], replicated, may hold values from 0.0005 to 0.005
- grain_param: float32 [128], replicated, may hold values from 0.1 to 10
- cycle_shifts: int32 [512], P('rad'), may hold values from 0 to 511
- fragment_bins: int32 [128, 128], replicated, may hold values from 0 to 127
- gas_map: int32 [512], P('rad'), may hold values from 0 to 1023, as said below
Outputs:
- dust_density_out: float32 [512, 512, 128], P('rad', 'az')
- dust_velocity_out: float32 [512, 512, 2, 128], P('rad', 'az')
- gas_velocity_out: float32 [1024, 2, 2048], P('rad', None, 'az')
The draws below stay inside these ranges and needn't reach their ends.
Inputs may be any that keep to these rules, and one draw needn't show every extreme that they name: gas_map never decreases along the dust cycles; the first dust cycle maps to gas cycle 0 and the last to gas cycle 1024 - 1. `gas_map`: the dust cycles of index i of rad map into gas cycles of index i - 1 or i of rad, and each index after the first has a dust cycle in the gas cycles of index i - 1.
All inputs are finite; a program needn't handle non-finite values.
Results may differ from the reference program's by a relative error of at most 0.000064.
Values sent between devices are 32-bit elements; how exact they have to be, the bound alone decides.
No kernel may reach another device: no remote copies, remote signals or barrier semaphores. Data moves between devices by JAX's collectives and lax.ppermute only.
A program may use at most 64 MiB of HBM per device.

```python
import math
import jax
import jax.numpy as jnp
from jax import lax

NB = 128
RD = 64
GR = 128
NRD = 512
NPHI = 512
NRG = 1024
NGP = 2048


def draw_gas_map(key, part):
    radial_count = NRD // RD
    steps = jax.random.randint(jax.random.fold_in(key, 11), (radial_count, RD), 1, 8, dtype=jnp.int32)
    before = jnp.cumsum(steps, axis=1) - steps
    total = jnp.maximum(before[:, -1:], 1)
    index = jnp.arange(radial_count, dtype=jnp.int32)
    starts = jnp.where(index == 0, 0, index * GR - GR // 2).astype(jnp.int32)
    ends = jnp.where(index == radial_count - 1, NRG - 1, (index + 1) * GR - GR // 2).astype(jnp.int32)
    mapped = starts[:, None] + before * (ends - starts)[:, None] // total
    return mapped.reshape(NRD).astype(jnp.int32)


def with_ends(entries, rng, smallest, high):
    index_at = [jax.random.randint(jax.random.fold_in(rng, axis), (), 0, length) for axis, length in enumerate(entries.shape)]
    main_axis = entries.shape.index(max(entries.shape))
    beside = index_at[:main_axis] + [(index_at[main_axis] + 1) % entries.shape[main_axis]] + index_at[main_axis + 1:]
    return entries.at[tuple(index_at)].set(smallest).at[tuple(beside)].set(high)


def level_of(own_key, dims, shards, least, largest):
    def one(position, shards_of):
        steps = jax.random.uniform(jax.random.fold_in(jax.random.fold_in(own_key, 6), position), (shards_of,), jnp.float32, least / len(shards), largest / len(shards))
        return jnp.repeat(jnp.exp(steps), dims[position] // shards_of).reshape((-1,) + (1,) * (len(dims) - position - 1))

    level = one(*shards[0])
    for cut in shards[1:]:
        level = level * one(*cut)
    return level


def noise(key, shape, scale, most, split=(), kind=jnp.bfloat16):
    loudness = level_of(key, shape, split, -0.22, 0.18) if split else 1.0
    array = jax.random.normal(key, shape, jnp.float32) * scale * loudness
    return jnp.minimum(jnp.maximum(array, -most), most).astype(kind)


def setup_inputs(seed: int = 0) -> dict:
    splits = jax.random.split(jax.random.key(seed), 10)
    return {
        "dust_density": jnp.clip(jnp.exp(math.log(1.0) - 2.9957323 * jax.random.uniform(splits[0], (NRD, NPHI, NB), jnp.float32) ** level_of(splits[0], (NRD, NPHI, NB), ((0, 8), (1, 32)), -0.2, 0.2)), 0.05, 1.0),
        "dust_velocity": noise(splits[1], (NRD, NPHI, 2, NB), 1.0, 6.0, ((0, 8), (1, 32)), jnp.float32),
        "gas_density": jnp.clip(jnp.exp(math.log(2.0) - 1.3862944 * jax.random.uniform(splits[2], (NRG, NGP), jnp.float32) ** level_of(splits[2], (NRG, NGP), ((0, 8), (1, 32)), -0.2, 0.2)), 0.5, 2.0),
        "gas_velocity": noise(splits[3], (NRG, 2, NGP), 1.0, 6.0, ((0, 8), (2, 32)), jnp.float32),
        "kernel": jnp.clip(jnp.exp(jax.random.uniform(splits[4], (NB, NB), jnp.float32, math.log(0.0005), math.log(0.005))), 0.0005, 0.005),
        "grain_param": jnp.clip(jnp.exp(jax.random.uniform(splits[5], (NB,), jnp.float32, math.log(0.1), math.log(10.0))), 0.1, 10.0),
        "cycle_shifts": with_ends(jax.random.randint(splits[6], (NRD,), 0, NPHI), jax.random.fold_in(splits[6], 1), 0, NPHI - 1).astype(jnp.int32),
        "fragment_bins": with_ends(jax.random.randint(splits[7], (NB, NB), 0, NB), jax.random.fold_in(splits[7], 1), 0, NB - 1).astype(jnp.int32),
        "gas_map": draw_gas_map(jax.random.fold_in(splits[9], 71), 0),
    }


def reference(dust_density, dust_velocity, gas_density, gas_velocity, kernel, grain_param, cycle_shifts, fragment_bins, gas_map):
    nrd, nphi, nb = dust_density.shape
    nrg = gas_density.shape[0]
    index = ((jnp.arange(nphi, dtype=jnp.int32)[None, :] - cycle_shifts[:, None]) % nphi).astype(jnp.int32)
    moved_density = jnp.take_along_axis(dust_density, index[:, :, None], axis=1)
    moved_velocity = jnp.take_along_axis(dust_velocity, index[:, :, None, None], axis=1)
    onehot = (fragment_bins.reshape(-1)[:, None] == jnp.arange(nb, dtype=jnp.int32)[None, :]).astype(jnp.float32)
    table = kernel.reshape(-1)[:, None] * onehot
    cells = nrd * nphi
    block = math.gcd(cells, 1024)

    def coag_block(dens):
        pairs = (dens[:, :, None] * dens[:, None, :]).reshape(dens.shape[0], -1)
        gain = jnp.dot(pairs, table, precision=lax.Precision.HIGHEST)
        loss = dens * jnp.dot(dens, kernel.T, precision=lax.Precision.HIGHEST)
        return dens + gain - loss

    coag_density = lax.map(coag_block, moved_density.reshape(cells // block, block, nb)).reshape(nrd, nphi, nb)
    coarse_density = gas_density.reshape(nrg, nphi, 4).mean(-1)
    coarse_velocity = gas_velocity.reshape(nrg, 2, nphi, 4).mean(-1)
    rho_dust = coarse_density[gas_map]
    u_dust = jnp.transpose(coarse_velocity[gas_map], (0, 2, 1))
    frac = 1.0 - jnp.exp(-rho_dust[:, :, None] / grain_param[None, None, :])
    velocity_out = moved_velocity + (u_dust[:, :, :, None] - moved_velocity) * frac[:, :, None, :]
    momentum = jnp.sum(coag_density[:, :, None, :] * (velocity_out - moved_velocity), axis=3) / nb
    kick = jax.ops.segment_sum(momentum, gas_map, nrg)
    kick = jnp.repeat(jnp.transpose(kick, (0, 2, 1)), 4, axis=2)
    gas_out = gas_velocity - kick / gas_density[:, None, :]
    return coag_density, velocity_out, gas_out
```

```python
import math

import jax
import jax.numpy as jnp
from jax import lax
from jax.sharding import PartitionSpec as P
from jax.experimental import pallas as pl
from jax.experimental.pallas import tpu as pltpu
import functools

F32 = jnp.float32
BF16 = jnp.bfloat16


def split(x):
    hi = x.astype(BF16)
    lo = (x - hi.astype(F32)).astype(BF16)
    return hi, lo


def dot3(a, b):
    a_hi, a_lo = a
    b_hi, b_lo = b
    d = functools.partial(jnp.dot, preferred_element_type=F32)
    return d(a_hi, b_hi) + (d(a_hi, b_lo) + d(a_lo, b_hi))


def coag_kernel(n_ref, k_ref, f_ref, o_ref, nt_ref, gain_ref):
    bins = k_ref.shape[0]
    nt = n_ref[...].T
    nt_ref[...] = nt
    n_parts = split(nt)
    loss = nt * dot3(split(k_ref[...]), n_parts)
    gain_ref[...] = jnp.zeros_like(gain_ref)
    rows = lax.broadcasted_iota(jnp.int32, (bins, bins), 0)

    def step(i, carry):
        table = jnp.where(f_ref[pl.ds(i, 1), :] == rows, k_ref[pl.ds(i, 1), :], 0.0)
        gain_ref[...] += nt_ref[pl.ds(i, 1), :] * dot3(split(table), n_parts)
        return carry

    lax.fori_loop(0, bins, step, 0)
    o_ref[...] = (nt + gain_ref[...] - loss).T


def coag(dens, kernel, fragment_bins, block=512):
    cells, bins = dens.shape
    block = min(block, cells)
    return pl.pallas_call(
        coag_kernel,
        grid=(cells // block,),
        in_specs=[
            pl.BlockSpec((block, bins), lambda c: (c, 0)),
            pl.BlockSpec((bins, bins), lambda c: (0, 0)),
            pl.BlockSpec((bins, bins), lambda c: (0, 0)),
        ],
        out_specs=pl.BlockSpec((block, bins), lambda c: (c, 0)),
        out_shape=jax.ShapeDtypeStruct((cells, bins), F32),
        scratch_shapes=[pltpu.VMEM((bins, block), F32), pltpu.VMEM((bins, block), F32)],
    )(dens, kernel, fragment_bins)


def from_behind(block, axis, distance):
    devices = range(lax.axis_size(axis))
    route = [((i - distance) % len(devices), i) for i in devices]
    return lax.ppermute(block, axis, route)


def shifted(block, axis, distance):
    devices = range(lax.axis_size(axis))
    route = [(i - distance, i) for i in devices if i - distance in devices]
    return lax.ppermute(block, axis, route)


def body(
    dust_density,
    dust_velocity,
    gas_density,
    gas_velocity,
    kernel,
    grain_param,
    cycle_shifts,
    fragment_bins,
    gas_map,
):
    cycles, cells, bins = dust_density.shape
    gas_cycles = gas_density.shape[0]
    coag_local = coag(dust_density.reshape(cycles * cells, bins), kernel, fragment_bins)
    state = jnp.concatenate([coag_local.reshape(cycles, cells, 1, bins), dust_velocity], axis=2)
    az_count = lax.axis_size("az")
    quotient = cycle_shifts // cells
    remain = cycle_shifts % cells
    for level in range(az_count.bit_length() - 1):
        moved = from_behind(state, "az", 1 << level)
        taken = quotient // (1 << level) % 2 == 1
        state = jnp.where(taken[:, None, None, None], moved, state)
    before = from_behind(state, "az", 1)
    joined = jnp.concatenate([before, state], axis=1)
    position = cells + jnp.arange(cells, dtype=jnp.int32)[None, :] - remain[:, None]
    state = jnp.take_along_axis(joined, position[:, :, None, None], axis=1)
    coag_density = state[:, :, 0, :]
    moved_velocity = state[:, :, 1:, :]
    coarse_density = gas_density.reshape(gas_cycles, cells, 4).mean(-1)
    coarse_velocity = (
        gas_velocity.reshape(gas_cycles, 2, cells, 4).mean(-1).reshape(gas_cycles, 2 * cells)
    )
    prev_density, prev_velocity = shifted((coarse_density, coarse_velocity), "rad", 1)
    near_density = jnp.concatenate([prev_density, coarse_density], axis=0)
    near_velocity = jnp.concatenate([prev_velocity, coarse_velocity], axis=0)
    first_row = (lax.axis_index("rad") - 1) * gas_cycles
    near_rows = first_row + jnp.arange(2 * gas_cycles, dtype=jnp.int32)
    select = (gas_map[:, None] == near_rows[None, :]).astype(jnp.float32)
    rho_dust = jnp.dot(select, near_density, precision=lax.Precision.HIGHEST)
    u_flat = jnp.dot(select, near_velocity, precision=lax.Precision.HIGHEST)
    u_dust = jnp.transpose(u_flat.reshape(cycles, 2, cells), (0, 2, 1))
    frac = 1.0 - jnp.exp(-rho_dust[:, :, None] / grain_param[None, None, :])
    velocity_out = moved_velocity + (u_dust[:, :, :, None] - moved_velocity) * frac[:, :, None, :]
    momentum = jnp.sum(coag_density[:, :, None, :] * (velocity_out - moved_velocity), axis=3) / bins
    spread = jnp.repeat(jnp.transpose(momentum, (0, 2, 1)), 4, axis=2).reshape(cycles, 8 * cells)
    near_kick = jnp.dot(select.T, spread, precision=lax.Precision.HIGHEST)
    from_next = shifted(near_kick[:gas_cycles], "rad", -1)
    kick = (near_kick[gas_cycles:] + from_next).reshape(gas_cycles, 2, 4 * cells)
    gas_out = gas_velocity - kick / gas_density[:, None, :]
    return (coag_density, velocity_out, gas_out)


def solution(mesh):
    placed = (
        P("rad", "az", None),
        P("rad", "az", None, None),
        P("rad", "az"),
        P("rad", None, "az"),
        P(),
        P(),
        P("rad"),
        P(),
        P("rad"),
    )
    return jax.shard_map(
        body,
        mesh=mesh,
        in_specs=placed,
        out_specs=(P("rad", "az", None), P("rad", "az", None, None), P("rad", None, "az")),
        check_vma=False,
    )
```

```python
import math

import jax
import jax.numpy as jnp
from jax import lax
from jax.sharding import PartitionSpec as P
from jax.experimental import pallas as pl
from jax.experimental.pallas import tpu as pltpu
import functools

F32 = jnp.float32
BF16 = jnp.bfloat16


def split(x):
    hi = x.astype(BF16)
    lo = (x - hi.astype(F32)).astype(BF16)
    return hi, lo


def dot3(a, b):
    a_hi, a_lo = a
    b_hi, b_lo = b
    d = functools.partial(jnp.dot, preferred_element_type=F32)
    return d(a_hi, b_hi) + (d(a_hi, b_lo) + d(a_lo, b_hi))


def coag_kernel(n_ref, k_ref, f_ref, o_ref, nt_ref, gain_ref):
    bins = k_ref.shape[0]
    nt = n_ref[...].T
    nt_ref[...] = nt
    n_parts = split(nt)
    loss = nt * dot3(split(k_ref[...]), n_parts)
    gain_ref[...] = jnp.zeros_like(gain_ref)
    rows = lax.broadcasted_iota(jnp.int32, (bins, bins), 0)

    def step(i, carry):
        table = jnp.where(f_ref[pl.ds(i, 1), :] == rows, k_ref[pl.ds(i, 1), :], 0.0)
        gain_ref[...] += nt_ref[pl.ds(i, 1), :] * dot3(split(table), n_parts)
        return carry

    lax.fori_loop(0, bins, step, 0)
    o_ref[...] = (nt + gain_ref[...] - loss).T


def coag(dens, kernel, fragment_bins, block=512):
    cells, bins = dens.shape
    block = min(block, cells)
    return pl.pallas_call(
        coag_kernel,
        grid=(cells // block,),
        in_specs=[
            pl.BlockSpec((block, bins), lambda c: (c, 0)),
            pl.BlockSpec((bins, bins), lambda c: (0, 0)),
            pl.BlockSpec((bins, bins), lambda c: (0, 0)),
        ],
        out_specs=pl.BlockSpec((block, bins), lambda c: (c, 0)),
        out_shape=jax.ShapeDtypeStruct((cells, bins), F32),
        scratch_shapes=[pltpu.VMEM((bins, block), F32), pltpu.VMEM((bins, block), F32)],
    )(dens, kernel, fragment_bins)


def from_behind(block, axis, distance):
    devices = range(lax.axis_size(axis))
    route = [((i - distance) % len(devices), i) for i in devices]
    return lax.ppermute(block, axis, route)


def shifted(block, axis, distance):
    devices = range(lax.axis_size(axis))
    route = [(i - distance, i) for i in devices if i - distance in devices]
    return lax.ppermute(block, axis, route)


def body(
    dust_density,
    dust_velocity,
    gas_density,
    gas_velocity,
    kernel,
    grain_param,
    cycle_shifts,
    fragment_bins,
    gas_map,
):
    cycles, cells, bins = dust_density.shape
    gas_cycles = gas_density.shape[0]
    coag_local = coag(dust_density.reshape(cycles * cells, bins), kernel, fragment_bins)
    state = jnp.concatenate([coag_local.reshape(cycles, cells, 1, bins), dust_velocity], axis=2)
    az_count = lax.axis_size("az")
    whole = cells * az_count
    own = cycles // az_count
    rings = lax.all_to_all(state, "az", 0, 1, tiled=True)
    turns = lax.dynamic_slice(cycle_shifts, (lax.axis_index("az") * own,), (own,))
    doubled = jnp.concatenate([rings, rings], axis=1)
    rings = jnp.stack(
        [lax.dynamic_slice_in_dim(doubled[c], whole - turns[c], whole, 0) for c in range(own)]
    )
    state = lax.all_to_all(rings, "az", 1, 0, tiled=True)
    coag_density = state[:, :, 0, :]
    moved_velocity = state[:, :, 1:, :]
    coarse_density = gas_density.reshape(gas_cycles, cells, 4).mean(-1)
    coarse_velocity = (
        gas_velocity.reshape(gas_cycles, 2, cells, 4).mean(-1).reshape(gas_cycles, 2 * cells)
    )
    prev_density, prev_velocity = shifted((coarse_density, coarse_velocity), "rad", 1)
    near_density = jnp.concatenate([prev_density, coarse_density], axis=0)
    near_velocity = jnp.concatenate([prev_velocity, coarse_velocity], axis=0)
    first_row = (lax.axis_index("rad") - 1) * gas_cycles
    near_rows = first_row + jnp.arange(2 * gas_cycles, dtype=jnp.int32)
    select = (gas_map[:, None] == near_rows[None, :]).astype(jnp.float32)
    rho_dust = jnp.dot(select, near_density, precision=lax.Precision.HIGHEST)
    u_flat = jnp.dot(select, near_velocity, precision=lax.Precision.HIGHEST)
    u_dust = jnp.transpose(u_flat.reshape(cycles, 2, cells), (0, 2, 1))
    frac = 1.0 - jnp.exp(-rho_dust[:, :, None] / grain_param[None, None, :])
    velocity_out = moved_velocity + (u_dust[:, :, :, None] - moved_velocity) * frac[:, :, None, :]
    momentum = jnp.sum(coag_density[:, :, None, :] * (velocity_out - moved_velocity), axis=3) / bins
    spread = jnp.repeat(jnp.transpose(momentum, (0, 2, 1)), 4, axis=2).reshape(cycles, 8 * cells)
    near_kick = jnp.dot(select.T, spread, precision=lax.Precision.HIGHEST)
    from_next = shifted(near_kick[:gas_cycles], "rad", -1)
    kick = (near_kick[gas_cycles:] + from_next).reshape(gas_cycles, 2, 4 * cells)
    gas_out = gas_velocity - kick / gas_density[:, None, :]
    return (coag_density, velocity_out, gas_out)


def solution(mesh):
    placed = (
        P("rad", "az", None),
        P("rad", "az", None, None),
        P("rad", "az"),
        P("rad", None, "az"),
        P(),
        P(),
        P("rad"),
        P(),
        P("rad"),
    )
    return jax.shard_map(
        body,
        mesh=mesh,
        in_specs=placed,
        out_specs=(P("rad", "az", None), P("rad", "az", None, None), P("rad", None, "az")),
        check_vma=False,
    )
```

```python
import math

import jax
import jax.numpy as jnp
from jax import lax
from jax.sharding import PartitionSpec as P
from jax.experimental import pallas as pl
from jax.experimental.pallas import tpu as pltpu
import functools

F32 = jnp.float32
BF16 = jnp.bfloat16


def split(x):
    hi = x.astype(BF16)
    lo = (x - hi.astype(F32)).astype(BF16)
    return hi, lo


def dot3(a, b):
    a_hi, a_lo = a
    b_hi, b_lo = b
    d = functools.partial(jnp.dot, preferred_element_type=F32)
    return d(a_hi, b_hi) + (d(a_hi, b_lo) + d(a_lo, b_hi))


def coag_kernel(n_ref, k_ref, f_ref, o_ref, nt_ref, gain_ref):
    bins = k_ref.shape[0]
    nt = n_ref[...].T
    nt_ref[...] = nt
    n_parts = split(nt)
    loss = nt * dot3(split(k_ref[...]), n_parts)
    gain_ref[...] = jnp.zeros_like(gain_ref)
    rows = lax.broadcasted_iota(jnp.int32, (bins, bins), 0)

    def step(i, carry):
        table = jnp.where(f_ref[pl.ds(i, 1), :] == rows, k_ref[pl.ds(i, 1), :], 0.0)
        gain_ref[...] += nt_ref[pl.ds(i, 1), :] * dot3(split(table), n_parts)
        return carry

    lax.fori_loop(0, bins, step, 0)
    o_ref[...] = (nt + gain_ref[...] - loss).T


def coag(dens, kernel, fragment_bins, block=512):
    cells, bins = dens.shape
    block = min(block, cells)
    return pl.pallas_call(
        coag_kernel,
        grid=(cells // block,),
        in_specs=[
            pl.BlockSpec((block, bins), lambda c: (c, 0)),
            pl.BlockSpec((bins, bins), lambda c: (0, 0)),
            pl.BlockSpec((bins, bins), lambda c: (0, 0)),
        ],
        out_specs=pl.BlockSpec((block, bins), lambda c: (c, 0)),
        out_shape=jax.ShapeDtypeStruct((cells, bins), F32),
        scratch_shapes=[pltpu.VMEM((bins, block), F32), pltpu.VMEM((bins, block), F32)],
        cost_estimate=pl.CostEstimate(
            flops=6 * cells * bins**3, transcendentals=0, bytes_accessed=8 * cells * bins
        ),
    )(dens, kernel, fragment_bins)


def from_behind(block, axis, distance):
    devices = range(lax.axis_size(axis))
    route = [((i - distance) % len(devices), i) for i in devices]
    return lax.ppermute(block, axis, route)


def shifted(block, axis, distance):
    devices = range(lax.axis_size(axis))
    route = [(i - distance, i) for i in devices if i - distance in devices]
    return lax.ppermute(block, axis, route)


def body(
    dust_density,
    dust_velocity,
    gas_density,
    gas_velocity,
    kernel,
    grain_param,
    cycle_shifts,
    fragment_bins,
    gas_map,
):
    cycles, cells, bins = dust_density.shape
    gas_cycles = gas_density.shape[0]
    az_count = lax.axis_size("az")
    whole = cells * az_count
    own = cycles // az_count
    turns = lax.dynamic_slice(cycle_shifts, (lax.axis_index("az") * own,), (own,))
    ring_velocity = lax.all_to_all(dust_velocity, "az", 0, 1, tiled=True)
    coag_local = coag(dust_density.reshape(cycles * cells, bins), kernel, fragment_bins)
    coag_local, ring_velocity = lax.optimization_barrier((coag_local, ring_velocity))
    ring_density = lax.all_to_all(coag_local.reshape(cycles, cells, 1, bins), "az", 0, 1, tiled=True)
    rings = jnp.concatenate([ring_density, ring_velocity], axis=2)
    doubled = jnp.concatenate([rings, rings], axis=1)
    rings = jnp.stack(
        [lax.dynamic_slice_in_dim(doubled[c], whole - turns[c], whole, 0) for c in range(own)]
    )
    state = lax.all_to_all(rings, "az", 1, 0, tiled=True)
    coag_density = state[:, :, 0, :]
    moved_velocity = state[:, :, 1:, :]
    coarse_density = gas_density.reshape(gas_cycles, cells, 4).mean(-1)
    coarse_velocity = (
        gas_velocity.reshape(gas_cycles, 2, cells, 4).mean(-1).reshape(gas_cycles, 2 * cells)
    )
    prev_density, prev_velocity = shifted((coarse_density, coarse_velocity), "rad", 1)
    near_density = jnp.concatenate([prev_density, coarse_density], axis=0)
    near_velocity = jnp.concatenate([prev_velocity, coarse_velocity], axis=0)
    first_row = (lax.axis_index("rad") - 1) * gas_cycles
    near_rows = first_row + jnp.arange(2 * gas_cycles, dtype=jnp.int32)
    select = (gas_map[:, None] == near_rows[None, :]).astype(jnp.float32)
    rho_dust = jnp.dot(select, near_density, precision=lax.Precision.HIGHEST)
    u_flat = jnp.dot(select, near_velocity, precision=lax.Precision.HIGHEST)
    u_dust = jnp.transpose(u_flat.reshape(cycles, 2, cells), (0, 2, 1))
    frac = 1.0 - jnp.exp(-rho_dust[:, :, None] / grain_param[None, None, :])
    velocity_out = moved_velocity + (u_dust[:, :, :, None] - moved_velocity) * frac[:, :, None, :]
    momentum = jnp.sum(coag_density[:, :, None, :] * (velocity_out - moved_velocity), axis=3) / bins
    spread = jnp.repeat(jnp.transpose(momentum, (0, 2, 1)), 4, axis=2).reshape(cycles, 8 * cells)
    near_kick = jnp.dot(select.T, spread, precision=lax.Precision.HIGHEST)
    from_next = shifted(near_kick[:gas_cycles], "rad", -1)
    kick = (near_kick[gas_cycles:] + from_next).reshape(gas_cycles, 2, 4 * cells)
    gas_out = gas_velocity - kick / gas_density[:, None, :]
    return (coag_density, velocity_out, gas_out)


def solution(mesh):
    placed = (
        P("rad", "az", None),
        P("rad", "az", None, None),
        P("rad", "az"),
        P("rad", None, "az"),
        P(),
        P(),
        P("rad"),
        P(),
        P("rad"),
    )
    return jax.shard_map(
        body,
        mesh=mesh,
        in_specs=placed,
        out_specs=(P("rad", "az", None), P("rad", "az", None, None), P("rad", None, "az")),
        check_vma=False,
    )
```

```python
import math

import jax
import jax.numpy as jnp
from jax import lax
from jax.sharding import PartitionSpec as P
from jax.experimental import pallas as pl
from jax.experimental.pallas import tpu as pltpu
import functools

F32 = jnp.float32
BF16 = jnp.bfloat16


def split(x):
    hi = x.astype(BF16)
    lo = (x - hi.astype(F32)).astype(BF16)
    return hi, lo


def coag_kernel(n_ref, k_ref, f_ref, o_ref, nt_ref, gain_ref, rhs_ref, *, group):
    bins = k_ref.shape[0]
    nt = n_ref[...].T
    nt_ref[...] = nt
    n_hi, n_lo = split(nt)
    rhs_ref[...] = jnp.concatenate([n_hi, n_lo, n_hi], axis=0)

    def three_pass(table):
        t_hi, t_lo = split(table)
        lhs = jnp.concatenate([t_hi, t_hi, t_lo], axis=1)
        return jnp.dot(lhs, rhs_ref[...], preferred_element_type=F32)

    loss = nt * three_pass(k_ref[...])
    gain_ref[...] = jnp.zeros_like(gain_ref)
    rows = lax.broadcasted_iota(jnp.int32, (bins, bins), 0)

    def step(s, carry):
        first = s * group
        tables = [
            jnp.where(f_ref[pl.ds(first + g, 1), :] == rows, k_ref[pl.ds(first + g, 1), :], 0.0)
            for g in range(group)
        ]
        q = three_pass(jnp.concatenate(tables, axis=0))
        acc = gain_ref[...]
        for g in range(group):
            acc = acc + nt_ref[pl.ds(first + g, 1), :] * q[g * bins : (g + 1) * bins]
        gain_ref[...] = acc
        return carry

    lax.fori_loop(0, bins // group, step, 0)
    o_ref[...] = (nt + gain_ref[...] - loss).T


def coag(dens, kernel, fragment_bins, group=16):
    cells, bins = dens.shape
    full = lambda shape: pl.BlockSpec(shape, lambda c: (0, 0))
    return pl.pallas_call(
        functools.partial(coag_kernel, group=group),
        grid=(1,),
        in_specs=[full((cells, bins)), full((bins, bins)), full((bins, bins))],
        out_specs=full((cells, bins)),
        out_shape=jax.ShapeDtypeStruct((cells, bins), F32),
        scratch_shapes=[
            pltpu.VMEM((bins, cells), F32),
            pltpu.VMEM((bins, cells), F32),
            pltpu.VMEM((3 * bins, cells), BF16),
        ],
        cost_estimate=pl.CostEstimate(
            flops=6 * cells * bins**3, transcendentals=0, bytes_accessed=8 * cells * bins
        ),
    )(dens, kernel, fragment_bins)


def from_behind(block, axis, distance):
    devices = range(lax.axis_size(axis))
    route = [((i - distance) % len(devices), i) for i in devices]
    return lax.ppermute(block, axis, route)


def shifted(block, axis, distance):
    devices = range(lax.axis_size(axis))
    route = [(i - distance, i) for i in devices if i - distance in devices]
    return lax.ppermute(block, axis, route)


def body(
    dust_density,
    dust_velocity,
    gas_density,
    gas_velocity,
    kernel,
    grain_param,
    cycle_shifts,
    fragment_bins,
    gas_map,
):
    cycles, cells, bins = dust_density.shape
    gas_cycles = gas_density.shape[0]
    az_count = lax.axis_size("az")
    whole = cells * az_count
    own = cycles // az_count
    turns = lax.dynamic_slice(cycle_shifts, (lax.axis_index("az") * own,), (own,))
    ring_velocity = lax.all_to_all(dust_velocity, "az", 0, 1, tiled=True)
    coag_local = coag(dust_density.reshape(cycles * cells, bins), kernel, fragment_bins)
    coag_local, ring_velocity = lax.optimization_barrier((coag_local, ring_velocity))
    ring_density = lax.all_to_all(coag_local.reshape(cycles, cells, 1, bins), "az", 0, 1, tiled=True)
    rings = jnp.concatenate([ring_density, ring_velocity], axis=2)
    doubled = jnp.concatenate([rings, rings], axis=1)
    rings = jnp.stack(
        [lax.dynamic_slice_in_dim(doubled[c], whole - turns[c], whole, 0) for c in range(own)]
    )
    state = lax.all_to_all(rings, "az", 1, 0, tiled=True)
    coag_density = state[:, :, 0, :]
    moved_velocity = state[:, :, 1:, :]
    coarse_density = gas_density.reshape(gas_cycles, cells, 4).mean(-1)
    coarse_velocity = (
        gas_velocity.reshape(gas_cycles, 2, cells, 4).mean(-1).reshape(gas_cycles, 2 * cells)
    )
    prev_density, prev_velocity = shifted((coarse_density, coarse_velocity), "rad", 1)
    near_density = jnp.concatenate([prev_density, coarse_density], axis=0)
    near_velocity = jnp.concatenate([prev_velocity, coarse_velocity], axis=0)
    first_row = (lax.axis_index("rad") - 1) * gas_cycles
    near_rows = first_row + jnp.arange(2 * gas_cycles, dtype=jnp.int32)
    select = (gas_map[:, None] == near_rows[None, :]).astype(jnp.float32)
    rho_dust = jnp.dot(select, near_density, precision=lax.Precision.HIGHEST)
    u_flat = jnp.dot(select, near_velocity, precision=lax.Precision.HIGHEST)
    u_dust = jnp.transpose(u_flat.reshape(cycles, 2, cells), (0, 2, 1))
    frac = 1.0 - jnp.exp(-rho_dust[:, :, None] / grain_param[None, None, :])
    velocity_out = moved_velocity + (u_dust[:, :, :, None] - moved_velocity) * frac[:, :, None, :]
    momentum = jnp.sum(coag_density[:, :, None, :] * (velocity_out - moved_velocity), axis=3) / bins
    spread = jnp.repeat(jnp.transpose(momentum, (0, 2, 1)), 4, axis=2).reshape(cycles, 8 * cells)
    near_kick = jnp.dot(select.T, spread, precision=lax.Precision.HIGHEST)
    from_next = shifted(near_kick[:gas_cycles], "rad", -1)
    kick = (near_kick[gas_cycles:] + from_next).reshape(gas_cycles, 2, 4 * cells)
    gas_out = gas_velocity - kick / gas_density[:, None, :]
    return (coag_density, velocity_out, gas_out)


def solution(mesh):
    placed = (
        P("rad", "az", None),
        P("rad", "az", None, None),
        P("rad", "az"),
        P("rad", None, "az"),
        P(),
        P(),
        P("rad"),
        P(),
        P("rad"),
    )
    return jax.shard_map(
        body,
        mesh=mesh,
        in_specs=placed,
        out_specs=(P("rad", "az", None), P("rad", "az", None, None), P("rad", None, "az")),
        check_vma=False,
    )
```

```python
import math

import jax
import jax.numpy as jnp
from jax import lax
from jax.sharding import PartitionSpec as P
from jax.experimental import pallas as pl
from jax.experimental.pallas import tpu as pltpu
import functools

F32 = jnp.float32
BF16 = jnp.bfloat16


def split(x):
    hi = x.astype(BF16)
    lo = (x - hi.astype(F32)).astype(BF16)
    return hi, lo


def coag_kernel(n_ref, k_ref, f_ref, o_ref, nt_ref, gain_ref, rhs_ref, *, group):
    bins = k_ref.shape[0]
    nt = n_ref[...].T
    nt_ref[...] = nt
    n_hi, n_lo = split(nt)
    rhs_ref[...] = jnp.concatenate([n_hi, n_lo, n_hi], axis=0)

    def three_pass(table):
        t_hi, t_lo = split(table)
        lhs = jnp.concatenate([t_hi, t_hi, t_lo], axis=1)
        return jnp.dot(lhs, rhs_ref[...], preferred_element_type=F32)

    loss = nt * three_pass(k_ref[...])
    gain_ref[...] = jnp.zeros_like(gain_ref)
    rows = lax.broadcasted_iota(jnp.int32, (bins, bins), 0)

    def step(s, carry):
        first = s * group
        tables = [
            jnp.where(f_ref[pl.ds(first + g, 1), :] == rows, k_ref[pl.ds(first + g, 1), :], 0.0)
            for g in range(group)
        ]
        q = three_pass(jnp.concatenate(tables, axis=0))
        acc = gain_ref[...]
        for g in range(group):
            acc = acc + nt_ref[pl.ds(first + g, 1), :] * q[g * bins : (g + 1) * bins]
        gain_ref[...] = acc
        return carry

    lax.fori_loop(0, bins // group, step, 0)
    o_ref[...] = (nt + gain_ref[...] - loss).T


def coag(dens, kernel, fragment_bins, group=16):
    cells, bins = dens.shape
    full = lambda shape: pl.BlockSpec(shape, lambda c: (0, 0))
    return pl.pallas_call(
        functools.partial(coag_kernel, group=group),
        grid=(1,),
        in_specs=[full((cells, bins)), full((bins, bins)), full((bins, bins))],
        out_specs=full((cells, bins)),
        out_shape=jax.ShapeDtypeStruct((cells, bins), F32),
        scratch_shapes=[
            pltpu.VMEM((bins, cells), F32),
            pltpu.VMEM((bins, cells), F32),
            pltpu.VMEM((3 * bins, cells), BF16),
        ],
        cost_estimate=pl.CostEstimate(
            flops=6 * cells * bins**3, transcendentals=0, bytes_accessed=8 * cells * bins
        ),
    )(dens, kernel, fragment_bins)


def from_behind(block, axis, distance):
    devices = range(lax.axis_size(axis))
    route = [((i - distance) % len(devices), i) for i in devices]
    return lax.ppermute(block, axis, route)


def shifted(block, axis, distance):
    devices = range(lax.axis_size(axis))
    route = [(i - distance, i) for i in devices if i - distance in devices]
    return lax.ppermute(block, axis, route)


def body(
    dust_density,
    dust_velocity,
    gas_density,
    gas_velocity,
    kernel,
    grain_param,
    cycle_shifts,
    fragment_bins,
    gas_map,
):
    cycles, cells, bins = dust_density.shape
    gas_cycles = gas_density.shape[0]
    az_count = lax.axis_size("az")
    whole = cells * az_count
    own = cycles // az_count
    turns = lax.dynamic_slice(cycle_shifts, (lax.axis_index("az") * own,), (own,))
    state = jnp.concatenate([dust_density[:, :, None, :], dust_velocity], axis=2)
    rings = lax.all_to_all(state, "az", 0, 1, tiled=True)
    doubled = jnp.concatenate([rings, rings], axis=1)
    rings = jnp.stack(
        [lax.dynamic_slice_in_dim(doubled[c], whole - turns[c], whole, 0) for c in range(own)]
    )
    moved_velocity = lax.all_to_all(rings[:, :, 1:, :], "az", 1, 0, tiled=True)
    ring_coag = coag(rings[:, :, 0, :].reshape(own * whole, bins), kernel, fragment_bins)
    ring_coag, moved_velocity = lax.optimization_barrier((ring_coag, moved_velocity))
    coag_density = lax.all_to_all(ring_coag.reshape(own, whole, bins), "az", 1, 0, tiled=True)
    coarse_density = gas_density.reshape(gas_cycles, cells, 4).mean(-1)
    coarse_velocity = (
        gas_velocity.reshape(gas_cycles, 2, cells, 4).mean(-1).reshape(gas_cycles, 2 * cells)
    )
    prev_density, prev_velocity = shifted((coarse_density, coarse_velocity), "rad", 1)
    near_density = jnp.concatenate([prev_density, coarse_density], axis=0)
    near_velocity = jnp.concatenate([prev_velocity, coarse_velocity], axis=0)
    first_row = (lax.axis_index("rad") - 1) * gas_cycles
    near_rows = first_row + jnp.arange(2 * gas_cycles, dtype=jnp.int32)
    select = (gas_map[:, None] == near_rows[None, :]).astype(jnp.float32)
    rho_dust = jnp.dot(select, near_density, precision=lax.Precision.HIGHEST)
    u_flat = jnp.dot(select, near_velocity, precision=lax.Precision.HIGHEST)
    u_dust = jnp.transpose(u_flat.reshape(cycles, 2, cells), (0, 2, 1))
    frac = 1.0 - jnp.exp(-rho_dust[:, :, None] / grain_param[None, None, :])
    velocity_out = moved_velocity + (u_dust[:, :, :, None] - moved_velocity) * frac[:, :, None, :]
    momentum = jnp.sum(coag_density[:, :, None, :] * (velocity_out - moved_velocity), axis=3) / bins
    spread = jnp.repeat(jnp.transpose(momentum, (0, 2, 1)), 4, axis=2).reshape(cycles, 8 * cells)
    near_kick = jnp.dot(select.T, spread, precision=lax.Precision.HIGHEST)
    from_next = shifted(near_kick[:gas_cycles], "rad", -1)
    kick = (near_kick[gas_cycles:] + from_next).reshape(gas_cycles, 2, 4 * cells)
    gas_out = gas_velocity - kick / gas_density[:, None, :]
    return (coag_density, velocity_out, gas_out)


def solution(mesh):
    placed = (
        P("rad", "az", None),
        P("rad", "az", None, None),
        P("rad", "az"),
        P("rad", None, "az"),
        P(),
        P(),
        P("rad"),
        P(),
        P("rad"),
    )
    return jax.shard_map(
        body,
        mesh=mesh,
        in_specs=placed,
        out_specs=(P("rad", "az", None), P("rad", "az", None, None), P("rad", None, "az")),
        check_vma=False,
    )
```

```python
import math

import jax
import jax.numpy as jnp
from jax import lax
from jax.sharding import PartitionSpec as P
from jax.experimental import pallas as pl
from jax.experimental.pallas import tpu as pltpu
import functools

F32 = jnp.float32
BF16 = jnp.bfloat16


def split(x):
    hi = x.astype(BF16)
    lo = (x - hi.astype(F32)).astype(BF16)
    return hi, lo


def coag_kernel(n_ref, k_ref, f_ref, o_ref, nt_ref, gain_ref, rhs_ref, *, group):
    bins = k_ref.shape[0]
    nt = n_ref[...].T
    nt_ref[...] = nt
    n_hi, n_lo = split(nt)
    rhs_ref[...] = jnp.concatenate([n_hi, n_lo, n_hi], axis=0)

    def three_pass(table):
        t_hi, t_lo = split(table)
        lhs = jnp.concatenate([t_hi, t_hi, t_lo], axis=1)
        return jnp.dot(lhs, rhs_ref[...], preferred_element_type=F32)

    loss = nt * three_pass(k_ref[...])
    gain_ref[...] = jnp.zeros_like(gain_ref)
    rows = lax.broadcasted_iota(jnp.int32, (bins, bins), 0)

    def step(s, carry):
        first = s * group
        tables = [
            jnp.where(f_ref[pl.ds(first + g, 1), :] == rows, k_ref[pl.ds(first + g, 1), :], 0.0)
            for g in range(group)
        ]
        q = three_pass(jnp.concatenate(tables, axis=0))
        acc = gain_ref[...]
        for g in range(group):
            acc = acc + nt_ref[pl.ds(first + g, 1), :] * q[g * bins : (g + 1) * bins]
        gain_ref[...] = acc
        return carry

    lax.fori_loop(0, bins // group, step, 0)
    o_ref[...] = (nt + gain_ref[...] - loss).T


def coag(dens, kernel, fragment_bins, group=16):
    cells, bins = dens.shape
    full = lambda shape: pl.BlockSpec(shape, lambda c: (0, 0))
    return pl.pallas_call(
        functools.partial(coag_kernel, group=group),
        grid=(1,),
        in_specs=[full((cells, bins)), full((bins, bins)), full((bins, bins))],
        out_specs=full((cells, bins)),
        out_shape=jax.ShapeDtypeStruct((cells, bins), F32),
        scratch_shapes=[
            pltpu.VMEM((bins, cells), F32),
            pltpu.VMEM((bins, cells), F32),
            pltpu.VMEM((3 * bins, cells), BF16),
        ],
        cost_estimate=pl.CostEstimate(
            flops=6 * cells * bins**3, transcendentals=0, bytes_accessed=8 * cells * bins
        ),
    )(dens, kernel, fragment_bins)


def from_behind(block, axis, distance):
    devices = range(lax.axis_size(axis))
    route = [((i - distance) % len(devices), i) for i in devices]
    return lax.ppermute(block, axis, route)


def shifted(block, axis, distance):
    devices = range(lax.axis_size(axis))
    route = [(i - distance, i) for i in devices if i - distance in devices]
    return lax.ppermute(block, axis, route)


def body(
    dust_density,
    dust_velocity,
    gas_density,
    gas_velocity,
    kernel,
    grain_param,
    cycle_shifts,
    fragment_bins,
    gas_map,
):
    cycles, cells, bins = dust_density.shape
    gas_cycles = gas_density.shape[0]
    az_count = lax.axis_size("az")
    whole = cells * az_count
    own = cycles // az_count
    turns = lax.dynamic_slice(cycle_shifts, (lax.axis_index("az") * own,), (own,))
    ring_velocity = lax.all_to_all(dust_velocity, "az", 0, 1, tiled=True)
    coag_local = coag(dust_density.reshape(cycles * cells, bins), kernel, fragment_bins)
    coarse_density = gas_density.reshape(gas_cycles, cells, 4).mean(-1)
    coarse_velocity = (
        gas_velocity.reshape(gas_cycles, 2, cells, 4).mean(-1).reshape(gas_cycles, 2 * cells)
    )
    prev_density, prev_velocity = shifted((coarse_density, coarse_velocity), "rad", 1)
    coag_local, ring_velocity, prev_density, prev_velocity = lax.optimization_barrier(
        (coag_local, ring_velocity, prev_density, prev_velocity)
    )
    ring_density = lax.all_to_all(coag_local.reshape(cycles, cells, 1, bins), "az", 0, 1, tiled=True)
    rings = jnp.concatenate([ring_density, ring_velocity], axis=2)
    doubled = jnp.concatenate([rings, rings], axis=1)
    rings = jnp.stack(
        [lax.dynamic_slice_in_dim(doubled[c], whole - turns[c], whole, 0) for c in range(own)]
    )
    state = lax.all_to_all(rings, "az", 1, 0, tiled=True)
    coag_density = state[:, :, 0, :]
    moved_velocity = state[:, :, 1:, :]
    near_density = jnp.concatenate([prev_density, coarse_density], axis=0)
    near_velocity = jnp.concatenate([prev_velocity, coarse_velocity], axis=0)
    first_row = (lax.axis_index("rad") - 1) * gas_cycles
    near_rows = first_row + jnp.arange(2 * gas_cycles, dtype=jnp.int32)
    select = (gas_map[:, None] == near_rows[None, :]).astype(jnp.float32)
    rho_dust = jnp.dot(select, near_density, precision=lax.Precision.HIGHEST)
    u_flat = jnp.dot(select, near_velocity, precision=lax.Precision.HIGHEST)
    u_dust = jnp.transpose(u_flat.reshape(cycles, 2, cells), (0, 2, 1))
    frac = 1.0 - jnp.exp(-rho_dust[:, :, None] / grain_param[None, None, :])
    velocity_out = moved_velocity + (u_dust[:, :, :, None] - moved_velocity) * frac[:, :, None, :]
    momentum = jnp.sum(coag_density[:, :, None, :] * (velocity_out - moved_velocity), axis=3) / bins
    spread = jnp.repeat(jnp.transpose(momentum, (0, 2, 1)), 4, axis=2).reshape(cycles, 8 * cells)
    near_kick = jnp.dot(select.T, spread, precision=lax.Precision.HIGHEST)
    from_next = shifted(near_kick[:gas_cycles], "rad", -1)
    kick = (near_kick[gas_cycles:] + from_next).reshape(gas_cycles, 2, 4 * cells)
    gas_out = gas_velocity - kick / gas_density[:, None, :]
    return (coag_density, velocity_out, gas_out)


def solution(mesh):
    placed = (
        P("rad", "az", None),
        P("rad", "az", None, None),
        P("rad", "az"),
        P("rad", None, "az"),
        P(),
        P(),
        P("rad"),
        P(),
        P("rad"),
    )
    return jax.shard_map(
        body,
        mesh=mesh,
        in_specs=placed,
        out_specs=(P("rad", "az", None), P("rad", "az", None, None), P("rad", None, "az")),
        check_vma=False,
    )
```

```python
import math

import jax
import jax.numpy as jnp
from jax import lax
from jax.sharding import PartitionSpec as P
from jax.experimental import pallas as pl
from jax.experimental.pallas import tpu as pltpu
import functools

F32 = jnp.float32
BF16 = jnp.bfloat16


def split(x):
    hi = x.astype(BF16)
    lo = (x - hi.astype(F32)).astype(BF16)
    return hi, lo


def coag_kernel(n_ref, k_ref, f_ref, o_ref, nt_ref, gain_ref, rhs_ref, *, group):
    bins = k_ref.shape[0]
    nt = n_ref[...].T
    nt_ref[...] = nt
    n_hi, n_lo = split(nt)
    rhs_ref[...] = jnp.concatenate([n_hi, n_lo, n_hi], axis=0)

    def three_pass(table):
        t_hi, t_lo = split(table)
        lhs = jnp.concatenate([t_hi, t_hi, t_lo], axis=1)
        return jnp.dot(lhs, rhs_ref[...], preferred_element_type=F32)

    loss = nt * three_pass(k_ref[...])
    gain_ref[...] = jnp.zeros_like(gain_ref)
    rows = lax.broadcasted_iota(jnp.int32, (bins, bins), 0)

    def step(s, carry):
        first = s * group
        tables = [
            jnp.where(f_ref[pl.ds(first + g, 1), :] == rows, k_ref[pl.ds(first + g, 1), :], 0.0)
            for g in range(group)
        ]
        q = three_pass(jnp.concatenate(tables, axis=0))
        acc = gain_ref[...]
        for g in range(group):
            acc = acc + nt_ref[pl.ds(first + g, 1), :] * q[g * bins : (g + 1) * bins]
        gain_ref[...] = acc
        return carry

    lax.fori_loop(0, bins // group, step, 0)
    o_ref[...] = (nt + gain_ref[...] - loss).T


def coag(dens, kernel, fragment_bins, group=16):
    cells, bins = dens.shape
    full = lambda shape: pl.BlockSpec(shape, lambda c: (0, 0))
    return pl.pallas_call(
        functools.partial(coag_kernel, group=group),
        grid=(1,),
        in_specs=[full((cells, bins)), full((bins, bins)), full((bins, bins))],
        out_specs=full((cells, bins)),
        out_shape=jax.ShapeDtypeStruct((cells, bins), F32),
        scratch_shapes=[
            pltpu.VMEM((bins, cells), F32),
            pltpu.VMEM((bins, cells), F32),
            pltpu.VMEM((3 * bins, cells), BF16),
        ],
        cost_estimate=pl.CostEstimate(
            flops=6 * cells * bins**3, transcendentals=0, bytes_accessed=8 * cells * bins
        ),
    )(dens, kernel, fragment_bins)


def from_behind(block, axis, distance):
    devices = range(lax.axis_size(axis))
    route = [((i - distance) % len(devices), i) for i in devices]
    return lax.ppermute(block, axis, route)


def shifted(block, axis, distance):
    devices = range(lax.axis_size(axis))
    route = [(i - distance, i) for i in devices if i - distance in devices]
    return lax.ppermute(block, axis, route)


def gathered(block, count):
    cycles, cells, channels, bins = block.shape
    flat = lax.all_to_all(block.reshape(-1, bins), "az", 0, 0, tiled=True)
    parts = flat.reshape(count, cycles // count, cells, channels, bins)
    return jnp.transpose(parts, (1, 0, 2, 3, 4)).reshape(cycles // count, count * cells, channels, bins)


def body(
    dust_density,
    dust_velocity,
    gas_density,
    gas_velocity,
    kernel,
    grain_param,
    cycle_shifts,
    fragment_bins,
    gas_map,
):
    cycles, cells, bins = dust_density.shape
    gas_cycles = gas_density.shape[0]
    az_count = lax.axis_size("az")
    whole = cells * az_count
    own = cycles // az_count
    turns = lax.dynamic_slice(cycle_shifts, (lax.axis_index("az") * own,), (own,))
    ring_velocity = gathered(dust_velocity, az_count)
    coag_local = coag(dust_density.reshape(cycles * cells, bins), kernel, fragment_bins)
    coag_local, ring_velocity = lax.optimization_barrier((coag_local, ring_velocity))
    ring_density = gathered(coag_local.reshape(cycles, cells, 1, bins), az_count)
    rings = jnp.concatenate([ring_density, ring_velocity], axis=2)
    doubled = jnp.concatenate([rings, rings], axis=1)
    rings = jnp.stack(
        [lax.dynamic_slice_in_dim(doubled[c], whole - turns[c], whole, 0) for c in range(own)]
    )
    state = lax.all_to_all(rings, "az", 1, 0, tiled=True)
    coag_density = state[:, :, 0, :]
    moved_velocity = state[:, :, 1:, :]
    coarse_density = gas_density.reshape(gas_cycles, cells, 4).mean(-1)
    coarse_velocity = (
        gas_velocity.reshape(gas_cycles, 2, cells, 4).mean(-1).reshape(gas_cycles, 2 * cells)
    )
    prev_density, prev_velocity = shifted((coarse_density, coarse_velocity), "rad", 1)
    near_density = jnp.concatenate([prev_density, coarse_density], axis=0)
    near_velocity = jnp.concatenate([prev_velocity, coarse_velocity], axis=0)
    first_row = (lax.axis_index("rad") - 1) * gas_cycles
    near_rows = first_row + jnp.arange(2 * gas_cycles, dtype=jnp.int32)
    select = (gas_map[:, None] == near_rows[None, :]).astype(jnp.float32)
    rho_dust = jnp.dot(select, near_density, precision=lax.Precision.HIGHEST)
    u_flat = jnp.dot(select, near_velocity, precision=lax.Precision.HIGHEST)
    u_dust = jnp.transpose(u_flat.reshape(cycles, 2, cells), (0, 2, 1))
    frac = 1.0 - jnp.exp(-rho_dust[:, :, None] / grain_param[None, None, :])
    velocity_out = moved_velocity + (u_dust[:, :, :, None] - moved_velocity) * frac[:, :, None, :]
    momentum = jnp.sum(coag_density[:, :, None, :] * (velocity_out - moved_velocity), axis=3) / bins
    spread = jnp.repeat(jnp.transpose(momentum, (0, 2, 1)), 4, axis=2).reshape(cycles, 8 * cells)
    near_kick = jnp.dot(select.T, spread, precision=lax.Precision.HIGHEST)
    from_next = shifted(near_kick[:gas_cycles], "rad", -1)
    kick = (near_kick[gas_cycles:] + from_next).reshape(gas_cycles, 2, 4 * cells)
    gas_out = gas_velocity - kick / gas_density[:, None, :]
    return (coag_density, velocity_out, gas_out)


def solution(mesh):
    placed = (
        P("rad", "az", None),
        P("rad", "az", None, None),
        P("rad", "az"),
        P("rad", None, "az"),
        P(),
        P(),
        P("rad"),
        P(),
        P("rad"),
    )
    return jax.shard_map(
        body,
        mesh=mesh,
        in_specs=placed,
        out_specs=(P("rad", "az", None), P("rad", "az", None, None), P("rad", None, "az")),
        check_vma=False,
    )
```

```python
import math

import jax
import jax.numpy as jnp
from jax import lax
from jax.sharding import PartitionSpec as P
from jax.experimental import pallas as pl
from jax.experimental.pallas import tpu as pltpu
import functools

F32 = jnp.float32
BF16 = jnp.bfloat16


def split(x):
    hi = x.astype(BF16)
    lo = (x - hi.astype(F32)).astype(BF16)
    return hi, lo


def coag_kernel(n_ref, k_ref, f_ref, o_ref, nt_ref, gain_ref, rhs_ref, *, group):
    bins = k_ref.shape[0]
    nt = n_ref[...].T
    nt_ref[...] = nt
    n_hi, n_lo = split(nt)
    rhs_ref[...] = jnp.concatenate([n_hi, n_lo, n_hi], axis=0)

    def three_pass(table):
        t_hi, t_lo = split(table)
        lhs = jnp.concatenate([t_hi, t_hi, t_lo], axis=1)
        return jnp.dot(lhs, rhs_ref[...], preferred_element_type=F32)

    loss = nt * three_pass(k_ref[...])
    gain_ref[...] = jnp.zeros_like(gain_ref)
    rows = lax.broadcasted_iota(jnp.int32, (bins, bins), 0)

    def step(s, carry):
        first = s * group
        tables = [
            jnp.where(f_ref[pl.ds(first + g, 1), :] == rows, k_ref[pl.ds(first + g, 1), :], 0.0)
            for g in range(group)
        ]
        q = three_pass(jnp.concatenate(tables, axis=0))
        acc = gain_ref[...]
        for g in range(group):
            acc = acc + nt_ref[pl.ds(first + g, 1), :] * q[g * bins : (g + 1) * bins]
        gain_ref[...] = acc
        return carry

    lax.fori_loop(0, bins // group, step, 0)
    o_ref[...] = (nt + gain_ref[...] - loss).T


def coag(dens, kernel, fragment_bins, group=16):
    cells, bins = dens.shape
    full = lambda shape: pl.BlockSpec(shape, lambda c: (0, 0))
    return pl.pallas_call(
        functools.partial(coag_kernel, group=group),
        grid=(1,),
        in_specs=[full((cells, bins)), full((bins, bins)), full((bins, bins))],
        out_specs=full((cells, bins)),
        out_shape=jax.ShapeDtypeStruct((cells, bins), F32),
        scratch_shapes=[
            pltpu.VMEM((bins, cells), F32),
            pltpu.VMEM((bins, cells), F32),
            pltpu.VMEM((3 * bins, cells), BF16),
        ],
        cost_estimate=pl.CostEstimate(
            flops=6 * cells * bins**3, transcendentals=0, bytes_accessed=8 * cells * bins
        ),
    )(dens, kernel, fragment_bins)


def from_behind(block, axis, distance):
    devices = range(lax.axis_size(axis))
    route = [((i - distance) % len(devices), i) for i in devices]
    return lax.ppermute(block, axis, route)


def shifted(block, axis, distance):
    devices = range(lax.axis_size(axis))
    route = [(i - distance, i) for i in devices if i - distance in devices]
    return lax.ppermute(block, axis, route)


def gathered(block, count):
    cycles, cells, channels, bins = block.shape
    flat = lax.all_to_all(block.reshape(-1, bins), "az", 0, 0, tiled=True)
    parts = flat.reshape(count, cycles // count, cells, channels, bins)
    return jnp.transpose(parts, (1, 0, 2, 3, 4)).reshape(cycles // count, count * cells, channels, bins)


def body(
    dust_density,
    dust_velocity,
    gas_density,
    gas_velocity,
    kernel,
    grain_param,
    cycle_shifts,
    fragment_bins,
    gas_map,
):
    cycles, cells, bins = dust_density.shape
    gas_cycles = gas_density.shape[0]
    az_count = lax.axis_size("az")
    whole = cells * az_count
    own = cycles // az_count
    turns = lax.dynamic_slice(cycle_shifts, (lax.axis_index("az") * own,), (own,))
    ring_velocity = gathered(dust_velocity, az_count)
    coag_local = coag(dust_density.reshape(cycles * cells, bins), kernel, fragment_bins)
    coag_local, ring_velocity = lax.optimization_barrier((coag_local, ring_velocity))
    ring_density = gathered(coag_local.reshape(cycles, cells, 1, bins), az_count)
    rings = jnp.concatenate([ring_density, ring_velocity], axis=2)
    doubled = jnp.concatenate([rings, rings], axis=1)
    rings = jnp.stack(
        [lax.dynamic_slice_in_dim(doubled[c], whole - turns[c], whole, 0) for c in range(own)]
    )
    state = lax.all_to_all(rings, "az", 1, 0, tiled=True)
    coag_density = state[:, :, 0, :]
    moved_velocity = state[:, :, 1:, :]
    coarse_density = gas_density.reshape(gas_cycles, cells, 4).mean(-1)
    coarse_velocity = (
        gas_velocity.reshape(gas_cycles, 2, cells, 4).mean(-1).reshape(gas_cycles, 2 * cells)
    )
    prev_density, prev_velocity = shifted((coarse_density, coarse_velocity), "rad", 1)
    near_density = jnp.concatenate([prev_density, coarse_density], axis=0)
    near_velocity = jnp.concatenate([prev_velocity, coarse_velocity], axis=0)
    first_row = (lax.axis_index("rad") - 1) * gas_cycles
    near_rows = first_row + jnp.arange(2 * gas_cycles, dtype=jnp.int32)
    select = (gas_map[:, None] == near_rows[None, :]).astype(jnp.float32)
    rho_dust = jnp.dot(select, near_density, precision=lax.Precision.HIGHEST)
    u_flat = jnp.dot(select, near_velocity, precision=lax.Precision.HIGHEST)
    u_dust = jnp.transpose(u_flat.reshape(cycles, 2, cells), (0, 2, 1))
    frac = 1.0 - jnp.exp(-rho_dust[:, :, None] / grain_param[None, None, :])
    velocity_out = moved_velocity + (u_dust[:, :, :, None] - moved_velocity) * frac[:, :, None, :]
    momentum = jnp.sum(coag_density[:, :, None, :] * (velocity_out - moved_velocity), axis=3) / bins
    by_axis = jnp.transpose(momentum, (0, 2, 1)).reshape(cycles, 2 * cells)
    message = jnp.concatenate([by_axis, gas_map.astype(F32)[:, None]], axis=1)
    arrived = shifted(message, "rad", -1)
    own_rows = near_rows[gas_cycles:]

    def kick_of(values, rows_of):
        spread = jnp.repeat(values.reshape(cycles, 2, cells), 4, axis=2).reshape(cycles, 8 * cells)
        hits = (rows_of[:, None] == own_rows[None, :]).astype(F32)
        return jnp.dot(hits.T, spread, precision=lax.Precision.HIGHEST)

    next_rows = arrived[:, 2 * cells].astype(jnp.int32)
    kick = kick_of(by_axis, gas_map) + kick_of(arrived[:, : 2 * cells], next_rows)
    kick = kick.reshape(gas_cycles, 2, 4 * cells)
    gas_out = gas_velocity - kick / gas_density[:, None, :]
    return (coag_density, velocity_out, gas_out)


def solution(mesh):
    placed = (
        P("rad", "az", None),
        P("rad", "az", None, None),
        P("rad", "az"),
        P("rad", None, "az"),
        P(),
        P(),
        P("rad"),
        P(),
        P("rad"),
    )
    return jax.shard_map(
        body,
        mesh=mesh,
        in_specs=placed,
        out_specs=(P("rad", "az", None), P("rad", "az", None, None), P("rad", None, "az")),
        check_vma=False,
    )
```

```python
import math

import jax
import jax.numpy as jnp
from jax import lax
from jax.sharding import PartitionSpec as P
from jax.experimental import pallas as pl
from jax.experimental.pallas import tpu as pltpu
import functools

F32 = jnp.float32
BF16 = jnp.bfloat16


def split(x):
    hi = x.astype(BF16)
    lo = (x - hi.astype(F32)).astype(BF16)
    return hi, lo


def coag_kernel(n_ref, k_ref, f_ref, o_ref, nt_ref, gain_ref, rhs_ref, *, group):
    bins = k_ref.shape[0]
    nt = n_ref[...].T
    nt_ref[...] = nt
    n_hi, n_lo = split(nt)
    rhs_ref[...] = jnp.concatenate([n_hi, n_lo, n_hi], axis=0)

    def three_pass(table):
        t_hi, t_lo = split(table)
        lhs = jnp.concatenate([t_hi, t_hi, t_lo], axis=1)
        return jnp.dot(lhs, rhs_ref[...], preferred_element_type=F32)

    loss = nt * three_pass(k_ref[...])
    gain_ref[...] = jnp.zeros_like(gain_ref)
    rows = lax.broadcasted_iota(jnp.int32, (bins, bins), 0)

    def step(s, carry):
        first = s * group
        tables = [
            jnp.where(f_ref[pl.ds(first + g, 1), :] == rows, k_ref[pl.ds(first + g, 1), :], 0.0)
            for g in range(group)
        ]
        q = three_pass(jnp.concatenate(tables, axis=0))
        acc = gain_ref[...]
        for g in range(group):
            acc = acc + nt_ref[pl.ds(first + g, 1), :] * q[g * bins : (g + 1) * bins]
        gain_ref[...] = acc
        return carry

    lax.fori_loop(0, bins // group, step, 0)
    o_ref[...] = (nt + gain_ref[...] - loss).T


def coag(dens, kernel, fragment_bins, group=16):
    cells, bins = dens.shape
    full = lambda shape: pl.BlockSpec(shape, lambda c: (0, 0))
    return pl.pallas_call(
        functools.partial(coag_kernel, group=group),
        grid=(1,),
        in_specs=[full((cells, bins)), full((bins, bins)), full((bins, bins))],
        out_specs=full((cells, bins)),
        out_shape=jax.ShapeDtypeStruct((cells, bins), F32),
        scratch_shapes=[
            pltpu.VMEM((bins, cells), F32),
            pltpu.VMEM((bins, cells), F32),
            pltpu.VMEM((3 * bins, cells), BF16),
        ],
        cost_estimate=pl.CostEstimate(
            flops=6 * cells * bins**3, transcendentals=0, bytes_accessed=8 * cells * bins
        ),
    )(dens, kernel, fragment_bins)


def from_behind(block, axis, distance):
    devices = range(lax.axis_size(axis))
    route = [((i - distance) % len(devices), i) for i in devices]
    return lax.ppermute(block, axis, route)


def shifted(block, axis, distance):
    devices = range(lax.axis_size(axis))
    route = [(i - distance, i) for i in devices if i - distance in devices]
    return lax.ppermute(block, axis, route)


def gathered(block, count):
    cycles, cells, channels, bins = block.shape
    flat = lax.all_to_all(block.reshape(-1, bins), "az", 0, 0, tiled=True)
    parts = flat.reshape(count, cycles // count, cells, channels, bins)
    return jnp.transpose(parts, (1, 0, 2, 3, 4)).reshape(cycles // count, count * cells, channels, bins)


def body(
    dust_density,
    dust_velocity,
    gas_density,
    gas_velocity,
    kernel,
    grain_param,
    cycle_shifts,
    fragment_bins,
    gas_map,
):
    cycles, cells, bins = dust_density.shape
    gas_cycles = gas_density.shape[0]
    az_count = lax.axis_size("az")
    whole = cells * az_count
    own = cycles // az_count
    turns = lax.dynamic_slice(cycle_shifts, (lax.axis_index("az") * own,), (own,))
    ring_density = gathered(dust_density[:, :, None, :], az_count)
    ring_density, dust_velocity = lax.optimization_barrier((ring_density, dust_velocity))
    ring_velocity = gathered(dust_velocity, az_count)
    ring_coag = coag(ring_density.reshape(own * whole, bins), kernel, fragment_bins)
    ring_coag, ring_velocity = lax.optimization_barrier((ring_coag, ring_velocity))
    ring_density = ring_coag.reshape(own, whole, 1, bins)
    rings = jnp.concatenate([ring_density, ring_velocity], axis=2)
    doubled = jnp.concatenate([rings, rings], axis=1)
    rings = jnp.stack(
        [lax.dynamic_slice_in_dim(doubled[c], whole - turns[c], whole, 0) for c in range(own)]
    )
    state = lax.all_to_all(rings, "az", 1, 0, tiled=True)
    coag_density = state[:, :, 0, :]
    moved_velocity = state[:, :, 1:, :]
    coarse_density = gas_density.reshape(gas_cycles, cells, 4).mean(-1)
    coarse_velocity = (
        gas_velocity.reshape(gas_cycles, 2, cells, 4).mean(-1).reshape(gas_cycles, 2 * cells)
    )
    prev_density, prev_velocity = shifted((coarse_density, coarse_velocity), "rad", 1)
    near_density = jnp.concatenate([prev_density, coarse_density], axis=0)
    near_velocity = jnp.concatenate([prev_velocity, coarse_velocity], axis=0)
    first_row = (lax.axis_index("rad") - 1) * gas_cycles
    near_rows = first_row + jnp.arange(2 * gas_cycles, dtype=jnp.int32)
    select = (gas_map[:, None] == near_rows[None, :]).astype(jnp.float32)
    rho_dust = jnp.dot(select, near_density, precision=lax.Precision.HIGHEST)
    u_flat = jnp.dot(select, near_velocity, precision=lax.Precision.HIGHEST)
    u_dust = jnp.transpose(u_flat.reshape(cycles, 2, cells), (0, 2, 1))
    frac = 1.0 - jnp.exp(-rho_dust[:, :, None] / grain_param[None, None, :])
    velocity_out = moved_velocity + (u_dust[:, :, :, None] - moved_velocity) * frac[:, :, None, :]
    momentum = jnp.sum(coag_density[:, :, None, :] * (velocity_out - moved_velocity), axis=3) / bins
    by_axis = jnp.transpose(momentum, (0, 2, 1)).reshape(cycles, 2 * cells)
    message = jnp.concatenate([by_axis, gas_map.astype(F32)[:, None]], axis=1)
    arrived = shifted(message, "rad", -1)
    own_rows = near_rows[gas_cycles:]

    def kick_of(values, rows_of):
        spread = jnp.repeat(values.reshape(cycles, 2, cells), 4, axis=2).reshape(cycles, 8 * cells)
        hits = (rows_of[:, None] == own_rows[None, :]).astype(F32)
        return jnp.dot(hits.T, spread, precision=lax.Precision.HIGHEST)

    next_rows = arrived[:, 2 * cells].astype(jnp.int32)
    kick = kick_of(by_axis, gas_map) + kick_of(arrived[:, : 2 * cells], next_rows)
    kick = kick.reshape(gas_cycles, 2, 4 * cells)
    gas_out = gas_velocity - kick / gas_density[:, None, :]
    return (coag_density, velocity_out, gas_out)


def solution(mesh):
    placed = (
        P("rad", "az", None),
        P("rad", "az", None, None),
        P("rad", "az"),
        P("rad", None, "az"),
        P(),
        P(),
        P("rad"),
        P(),
        P("rad"),
    )
    return jax.shard_map(
        body,
        mesh=mesh,
        in_specs=placed,
        out_specs=(P("rad", "az", None), P("rad", "az", None, None), P("rad", None, "az")),
        check_vma=False,
    )
```

```python
import math

import jax
import jax.numpy as jnp
from jax import lax
from jax.sharding import PartitionSpec as P
from jax.experimental import pallas as pl
from jax.experimental.pallas import tpu as pltpu
import functools

F32 = jnp.float32
BF16 = jnp.bfloat16


def split(x):
    hi = x.astype(BF16)
    lo = (x - hi.astype(F32)).astype(BF16)
    return hi, lo


def coag_kernel(n_ref, k_ref, f_ref, o_ref, nt_ref, gain_ref, rhs_ref, *, group):
    bins = k_ref.shape[0]
    nt = n_ref[...].T
    nt_ref[...] = nt
    n_hi, n_lo = split(nt)
    rhs_ref[...] = jnp.concatenate([n_hi, n_lo, n_hi], axis=0)

    def three_pass(table):
        t_hi, t_lo = split(table)
        lhs = jnp.concatenate([t_hi, t_hi, t_lo], axis=1)
        return jnp.dot(lhs, rhs_ref[...], preferred_element_type=F32)

    loss = nt * three_pass(k_ref[...])
    gain_ref[...] = jnp.zeros_like(gain_ref)
    rows = lax.broadcasted_iota(jnp.int32, (bins, bins), 0)

    def step(s, carry):
        first = s * group
        tables = [
            jnp.where(f_ref[pl.ds(first + g, 1), :] == rows, k_ref[pl.ds(first + g, 1), :], 0.0)
            for g in range(group)
        ]
        q = three_pass(jnp.concatenate(tables, axis=0))
        acc = gain_ref[...]
        for g in range(group):
            acc = acc + nt_ref[pl.ds(first + g, 1), :] * q[g * bins : (g + 1) * bins]
        gain_ref[...] = acc
        return carry

    lax.fori_loop(0, bins // group, step, 0)
    o_ref[...] = (nt + gain_ref[...] - loss).T


def coag(dens, kernel, fragment_bins, group=16):
    cells, bins = dens.shape
    full = lambda shape: pl.BlockSpec(shape, lambda c: (0, 0))
    return pl.pallas_call(
        functools.partial(coag_kernel, group=group),
        grid=(1,),
        in_specs=[full((cells, bins)), full((bins, bins)), full((bins, bins))],
        out_specs=full((cells, bins)),
        out_shape=jax.ShapeDtypeStruct((cells, bins), F32),
        scratch_shapes=[
            pltpu.VMEM((bins, cells), F32),
            pltpu.VMEM((bins, cells), F32),
            pltpu.VMEM((3 * bins, cells), BF16),
        ],
        cost_estimate=pl.CostEstimate(
            flops=6 * cells * bins**3, transcendentals=0, bytes_accessed=8 * cells * bins
        ),
    )(dens, kernel, fragment_bins)


def from_behind(block, axis, distance):
    devices = range(lax.axis_size(axis))
    route = [((i - distance) % len(devices), i) for i in devices]
    return lax.ppermute(block, axis, route)


def shifted(block, axis, distance):
    devices = range(lax.axis_size(axis))
    route = [(i - distance, i) for i in devices if i - distance in devices]
    return lax.ppermute(block, axis, route)


def gathered(block, count):
    cycles, cells, channels, bins = block.shape
    flat = lax.all_to_all(block.reshape(-1, bins), "az", 0, 0, tiled=True)
    parts = flat.reshape(count, cycles // count, cells, channels, bins)
    return jnp.transpose(parts, (1, 0, 2, 3, 4)).reshape(cycles // count, count * cells, channels, bins)


def body(
    dust_density,
    dust_velocity,
    gas_density,
    gas_velocity,
    kernel,
    grain_param,
    cycle_shifts,
    fragment_bins,
    gas_map,
):
    cycles, cells, bins = dust_density.shape
    gas_cycles = gas_density.shape[0]
    az_count = lax.axis_size("az")
    whole = cells * az_count
    own = cycles // az_count
    turns = lax.dynamic_slice(cycle_shifts, (lax.axis_index("az") * own,), (own,))
    state = jnp.concatenate([dust_density[:, :, None, :], dust_velocity], axis=2)
    rings = gathered(state, az_count)

    def rolled(ring):
        doubled = jnp.concatenate([ring, ring], axis=1)
        return jnp.stack(
            [lax.dynamic_slice_in_dim(doubled[c], whole - turns[c], whole, 0) for c in range(own)]
        )

    moved_velocity = lax.all_to_all(rolled(rings[:, :, 1:, :]), "az", 1, 0, tiled=True)
    ring_coag = coag(rolled(rings[:, :, 0, :]).reshape(own * whole, bins), kernel, fragment_bins)
    coarse_density = gas_density.reshape(gas_cycles, cells, 4).mean(-1)
    coarse_velocity = (
        gas_velocity.reshape(gas_cycles, 2, cells, 4).mean(-1).reshape(gas_cycles, 2 * cells)
    )
    ring_coag, moved_velocity, coarse_density, coarse_velocity = lax.optimization_barrier(
        (ring_coag, moved_velocity, coarse_density, coarse_velocity)
    )
    coag_density = lax.all_to_all(ring_coag.reshape(own, whole, bins), "az", 1, 0, tiled=True)
    prev_density, prev_velocity = shifted((coarse_density, coarse_velocity), "rad", 1)
    near_density = jnp.concatenate([prev_density, coarse_density], axis=0)
    near_velocity = jnp.concatenate([prev_velocity, coarse_velocity], axis=0)
    first_row = (lax.axis_index("rad") - 1) * gas_cycles
    near_rows = first_row + jnp.arange(2 * gas_cycles, dtype=jnp.int32)
    select = (gas_map[:, None] == near_rows[None, :]).astype(jnp.float32)
    rho_dust = jnp.dot(select, near_density, precision=lax.Precision.HIGHEST)
    u_flat = jnp.dot(select, near_velocity, precision=lax.Precision.HIGHEST)
    u_dust = jnp.transpose(u_flat.reshape(cycles, 2, cells), (0, 2, 1))
    frac = 1.0 - jnp.exp(-rho_dust[:, :, None] / grain_param[None, None, :])
    velocity_out = moved_velocity + (u_dust[:, :, :, None] - moved_velocity) * frac[:, :, None, :]
    momentum = jnp.sum(coag_density[:, :, None, :] * (velocity_out - moved_velocity), axis=3) / bins
    by_axis = jnp.transpose(momentum, (0, 2, 1)).reshape(cycles, 2 * cells)
    message = jnp.concatenate([by_axis, gas_map.astype(F32)[:, None]], axis=1)
    arrived = shifted(message, "rad", -1)
    own_rows = near_rows[gas_cycles:]

    def kick_of(values, rows_of):
        spread = jnp.repeat(values.reshape(cycles, 2, cells), 4, axis=2).reshape(cycles, 8 * cells)
        hits = (rows_of[:, None] == own_rows[None, :]).astype(F32)
        return jnp.dot(hits.T, spread, precision=lax.Precision.HIGHEST)

    next_rows = arrived[:, 2 * cells].astype(jnp.int32)
    kick = kick_of(by_axis, gas_map) + kick_of(arrived[:, : 2 * cells], next_rows)
    kick = kick.reshape(gas_cycles, 2, 4 * cells)
    gas_out = gas_velocity - kick / gas_density[:, None, :]
    return (coag_density, velocity_out, gas_out)


def solution(mesh):
    placed = (
        P("rad", "az", None),
        P("rad", "az", None, None),
        P("rad", "az"),
        P("rad", None, "az"),
        P(),
        P(),
        P("rad"),
        P(),
        P("rad"),
    )
    return jax.shard_map(
        body,
        mesh=mesh,
        in_specs=placed,
        out_specs=(P("rad", "az", None), P("rad", "az", None, None), P("rad", None, "az")),
        check_vma=False,
    )
```

```python
import math

import jax
import jax.numpy as jnp
from jax import lax
from jax.sharding import PartitionSpec as P
from jax.experimental import pallas as pl
from jax.experimental.pallas import tpu as pltpu
import functools

F32 = jnp.float32
BF16 = jnp.bfloat16


def split(x):
    hi = x.astype(BF16)
    lo = (x - hi.astype(F32)).astype(BF16)
    return hi, lo


def coag_kernel(n_ref, k_ref, f_ref, o_ref, nt_ref, gain_ref, rhs_ref, *, group):
    bins = k_ref.shape[0]
    nt = n_ref[...].T
    nt_ref[...] = nt
    n_hi, n_lo = split(nt)
    rhs_ref[...] = jnp.concatenate([n_hi, n_lo, n_hi], axis=0)

    def three_pass(table):
        t_hi, t_lo = split(table)
        lhs = jnp.concatenate([t_hi, t_hi, t_lo], axis=1)
        return jnp.dot(lhs, rhs_ref[...], preferred_element_type=F32)

    loss = nt * three_pass(k_ref[...])
    gain_ref[...] = jnp.zeros_like(gain_ref)
    rows = lax.broadcasted_iota(jnp.int32, (bins, bins), 0)

    def step(s, carry):
        first = s * group
        tables = [
            jnp.where(f_ref[pl.ds(first + g, 1), :] == rows, k_ref[pl.ds(first + g, 1), :], 0.0)
            for g in range(group)
        ]
        q = three_pass(jnp.concatenate(tables, axis=0))
        acc = gain_ref[...]
        for g in range(group):
            acc = acc + nt_ref[pl.ds(first + g, 1), :] * q[g * bins : (g + 1) * bins]
        gain_ref[...] = acc
        return carry

    lax.fori_loop(0, bins // group, step, 0)
    o_ref[...] = (nt + gain_ref[...] - loss).T


def coag(dens, kernel, fragment_bins, group=16):
    cells, bins = dens.shape
    full = lambda shape: pl.BlockSpec(shape, lambda c: (0, 0))
    return pl.pallas_call(
        functools.partial(coag_kernel, group=group),
        grid=(1,),
        in_specs=[full((cells, bins)), full((bins, bins)), full((bins, bins))],
        out_specs=full((cells, bins)),
        out_shape=jax.ShapeDtypeStruct((cells, bins), F32),
        scratch_shapes=[
            pltpu.VMEM((bins, cells), F32),
            pltpu.VMEM((bins, cells), F32),
            pltpu.VMEM((3 * bins, cells), BF16),
        ],
        cost_estimate=pl.CostEstimate(
            flops=6 * cells * bins**3, transcendentals=0, bytes_accessed=8 * cells * bins
        ),
    )(dens, kernel, fragment_bins)


def from_behind(block, axis, distance):
    devices = range(lax.axis_size(axis))
    route = [((i - distance) % len(devices), i) for i in devices]
    return lax.ppermute(block, axis, route)


def shifted(block, axis, distance):
    devices = range(lax.axis_size(axis))
    route = [(i - distance, i) for i in devices if i - distance in devices]
    return lax.ppermute(block, axis, route)


def sent(block):
    return lax.all_to_all(block.reshape(-1, block.shape[-1]), "az", 0, 0, tiled=True)


def arranged(flat, cycles, cells, count):
    bins = flat.shape[-1]
    parts = flat.reshape(count, cycles // count, cells, -1, bins)
    return jnp.transpose(parts, (1, 0, 2, 3, 4)).reshape(cycles // count, count * cells, -1, bins)


def body(
    dust_density,
    dust_velocity,
    gas_density,
    gas_velocity,
    kernel,
    grain_param,
    cycle_shifts,
    fragment_bins,
    gas_map,
):
    cycles, cells, bins = dust_density.shape
    gas_cycles = gas_density.shape[0]
    az_count = lax.axis_size("az")
    whole = cells * az_count
    own = cycles // az_count
    turns = lax.dynamic_slice(cycle_shifts, (lax.axis_index("az") * own,), (own,))
    flat_velocity = sent(dust_velocity)
    coag_local = coag(dust_density.reshape(cycles * cells, bins), kernel, fragment_bins)
    coag_local, flat_velocity = lax.optimization_barrier((coag_local, flat_velocity))
    flat_density = sent(coag_local)
    flat_density, flat_velocity = lax.optimization_barrier((flat_density, flat_velocity))
    ring_velocity = arranged(flat_velocity, cycles, cells, az_count)
    ring_density = arranged(flat_density, cycles, cells, az_count)
    rings = jnp.concatenate([ring_density, ring_velocity], axis=2)
    doubled = jnp.concatenate([rings, rings], axis=1)
    rings = jnp.stack(
        [lax.dynamic_slice_in_dim(doubled[c], whole - turns[c], whole, 0) for c in range(own)]
    )
    state = lax.all_to_all(rings, "az", 1, 0, tiled=True)
    coag_density = state[:, :, 0, :]
    moved_velocity = state[:, :, 1:, :]
    coarse_density = gas_density.reshape(gas_cycles, cells, 4).mean(-1)
    coarse_velocity = (
        gas_velocity.reshape(gas_cycles, 2, cells, 4).mean(-1).reshape(gas_cycles, 2 * cells)
    )
    prev_density, prev_velocity = shifted((coarse_density, coarse_velocity), "rad", 1)
    near_density = jnp.concatenate([prev_density, coarse_density], axis=0)
    near_velocity = jnp.concatenate([prev_velocity, coarse_velocity], axis=0)
    first_row = (lax.axis_index("rad") - 1) * gas_cycles
    near_rows = first_row + jnp.arange(2 * gas_cycles, dtype=jnp.int32)
    select = (gas_map[:, None] == near_rows[None, :]).astype(jnp.float32)
    rho_dust = jnp.dot(select, near_density, precision=lax.Precision.HIGHEST)
    u_flat = jnp.dot(select, near_velocity, precision=lax.Precision.HIGHEST)
    u_dust = jnp.transpose(u_flat.reshape(cycles, 2, cells), (0, 2, 1))
    frac = 1.0 - jnp.exp(-rho_dust[:, :, None] / grain_param[None, None, :])
    velocity_out = moved_velocity + (u_dust[:, :, :, None] - moved_velocity) * frac[:, :, None, :]
    momentum = jnp.sum(coag_density[:, :, None, :] * (velocity_out - moved_velocity), axis=3) / bins
    by_axis = jnp.transpose(momentum, (0, 2, 1)).reshape(cycles, 2 * cells)
    message = jnp.concatenate([by_axis, gas_map.astype(F32)[:, None]], axis=1)
    arrived = shifted(message, "rad", -1)
    own_rows = near_rows[gas_cycles:]

    def kick_of(values, rows_of):
        spread = jnp.repeat(values.reshape(cycles, 2, cells), 4, axis=2).reshape(cycles, 8 * cells)
        hits = (rows_of[:, None] == own_rows[None, :]).astype(F32)
        return jnp.dot(hits.T, spread, precision=lax.Precision.HIGHEST)

    next_rows = arrived[:, 2 * cells].astype(jnp.int32)
    kick = kick_of(by_axis, gas_map) + kick_of(arrived[:, : 2 * cells], next_rows)
    kick = kick.reshape(gas_cycles, 2, 4 * cells)
    gas_out = gas_velocity - kick / gas_density[:, None, :]
    return (coag_density, velocity_out, gas_out)


def solution(mesh):
    placed = (
        P("rad", "az", None),
        P("rad", "az", None, None),
        P("rad", "az"),
        P("rad", None, "az"),
        P(),
        P(),
        P("rad"),
        P(),
        P("rad"),
    )
    return jax.shard_map(
        body,
        mesh=mesh,
        in_specs=placed,
        out_specs=(P("rad", "az", None), P("rad", "az", None, None), P("rad", None, "az")),
        check_vma=False,
    )
```

```python
import math

import jax
import jax.numpy as jnp
from jax import lax
from jax.sharding import PartitionSpec as P
from jax.experimental import pallas as pl
from jax.experimental.pallas import tpu as pltpu
import functools

F32 = jnp.float32
BF16 = jnp.bfloat16


def split(x):
    hi = x.astype(BF16)
    lo = (x - hi.astype(F32)).astype(BF16)
    return hi, lo


def coag_kernel(n_ref, k_ref, f_ref, o_ref, nt_ref, gain_ref, rhs_ref, *, group):
    bins = k_ref.shape[0]
    nt = n_ref[...].T
    nt_ref[...] = nt
    n_hi, n_lo = split(nt)
    rhs_ref[...] = jnp.concatenate([n_hi, n_lo, n_hi], axis=0)

    def three_pass(table):
        t_hi, t_lo = split(table)
        lhs = jnp.concatenate([t_hi, t_hi, t_lo], axis=1)
        return jnp.dot(lhs, rhs_ref[...], preferred_element_type=F32)

    loss = nt * three_pass(k_ref[...])
    gain_ref[...] = jnp.zeros_like(gain_ref)
    rows = lax.broadcasted_iota(jnp.int32, (bins, bins), 0)

    def step(s, carry):
        first = s * group
        tables = [
            jnp.where(f_ref[pl.ds(first + g, 1), :] == rows, k_ref[pl.ds(first + g, 1), :], 0.0)
            for g in range(group)
        ]
        q = three_pass(jnp.concatenate(tables, axis=0))
        acc = gain_ref[...]
        for g in range(group):
            acc = acc + nt_ref[pl.ds(first + g, 1), :] * q[g * bins : (g + 1) * bins]
        gain_ref[...] = acc
        return carry

    lax.fori_loop(0, bins // group, step, 0)
    o_ref[...] = (nt + gain_ref[...] - loss).T


def coag(dens, kernel, fragment_bins, group=16):
    cells, bins = dens.shape
    full = lambda shape: pl.BlockSpec(shape, lambda c: (0, 0))
    return pl.pallas_call(
        functools.partial(coag_kernel, group=group),
        grid=(1,),
        in_specs=[full((cells, bins)), full((bins, bins)), full((bins, bins))],
        out_specs=full((cells, bins)),
        out_shape=jax.ShapeDtypeStruct((cells, bins), F32),
        scratch_shapes=[
            pltpu.VMEM((bins, cells), F32),
            pltpu.VMEM((bins, cells), F32),
            pltpu.VMEM((3 * bins, cells), BF16),
        ],
        cost_estimate=pl.CostEstimate(
            flops=6 * cells * bins**3, transcendentals=0, bytes_accessed=8 * cells * bins
        ),
    )(dens, kernel, fragment_bins)


def from_behind(block, axis, distance):
    devices = range(lax.axis_size(axis))
    route = [((i - distance) % len(devices), i) for i in devices]
    return lax.ppermute(block, axis, route)


def shifted(block, axis, distance):
    devices = range(lax.axis_size(axis))
    route = [(i - distance, i) for i in devices if i - distance in devices]
    return lax.ppermute(block, axis, route)


def sent(block):
    return lax.all_to_all(block.reshape(-1, block.shape[-1]), "az", 0, 0, tiled=True)


def arranged(flat, cycles, cells, count):
    bins = flat.shape[-1]
    parts = flat.reshape(count, cycles // count, cells, -1, bins)
    return jnp.transpose(parts, (1, 0, 2, 3, 4)).reshape(cycles // count, count * cells, -1, bins)


def body(
    dust_density,
    dust_velocity,
    gas_density,
    gas_velocity,
    kernel,
    grain_param,
    cycle_shifts,
    fragment_bins,
    gas_map,
):
    cycles, cells, bins = dust_density.shape
    gas_cycles = gas_density.shape[0]
    az_count = lax.axis_size("az")
    whole = cells * az_count
    own = cycles // az_count
    turns = lax.dynamic_slice(cycle_shifts, (lax.axis_index("az") * own,), (own,))
    flat_velocity = sent(dust_velocity)
    coag_local = coag(dust_density.reshape(cycles * cells, bins), kernel, fragment_bins)
    coag_local, flat_velocity = lax.optimization_barrier((coag_local, flat_velocity))
    flat_density = sent(coag_local)
    flat_density, flat_velocity = lax.optimization_barrier((flat_density, flat_velocity))
    ring_velocity = arranged(flat_velocity, cycles, cells, az_count)
    ring_density = arranged(flat_density, cycles, cells, az_count)
    rings = jnp.concatenate([ring_density, ring_velocity], axis=2)
    doubled = jnp.concatenate([rings, rings], axis=1)
    rings = jnp.stack(
        [lax.dynamic_slice_in_dim(doubled[c], whole - turns[c], whole, 0) for c in range(own)],
        axis=1,
    )
    state = lax.all_to_all(rings.reshape(-1, bins), "az", 0, 0, tiled=True)
    state = state.reshape(az_count, cells, own, -1, bins)
    state = jnp.transpose(state, (0, 2, 1, 3, 4)).reshape(cycles, cells, -1, bins)
    coag_density = state[:, :, 0, :]
    moved_velocity = state[:, :, 1:, :]
    coarse_density = gas_density.reshape(gas_cycles, cells, 4).mean(-1)
    coarse_velocity = (
        gas_velocity.reshape(gas_cycles, 2, cells, 4).mean(-1).reshape(gas_cycles, 2 * cells)
    )
    prev_density, prev_velocity = shifted((coarse_density, coarse_velocity), "rad", 1)
    near_density = jnp.concatenate([prev_density, coarse_density], axis=0)
    near_velocity = jnp.concatenate([prev_velocity, coarse_velocity], axis=0)
    first_row = (lax.axis_index("rad") - 1) * gas_cycles
    near_rows = first_row + jnp.arange(2 * gas_cycles, dtype=jnp.int32)
    select = (gas_map[:, None] == near_rows[None, :]).astype(jnp.float32)
    rho_dust = jnp.dot(select, near_density, precision=lax.Precision.HIGHEST)
    u_flat = jnp.dot(select, near_velocity, precision=lax.Precision.HIGHEST)
    u_dust = jnp.transpose(u_flat.reshape(cycles, 2, cells), (0, 2, 1))
    frac = 1.0 - jnp.exp(-rho_dust[:, :, None] / grain_param[None, None, :])
    velocity_out = moved_velocity + (u_dust[:, :, :, None] - moved_velocity) * frac[:, :, None, :]
    momentum = jnp.sum(coag_density[:, :, None, :] * (velocity_out - moved_velocity), axis=3) / bins
    by_axis = jnp.transpose(momentum, (0, 2, 1)).reshape(cycles, 2 * cells)
    message = jnp.concatenate([by_axis, gas_map.astype(F32)[:, None]], axis=1)
    arrived = shifted(message, "rad", -1)
    own_rows = near_rows[gas_cycles:]

    def kick_of(values, rows_of):
        spread = jnp.repeat(values.reshape(cycles, 2, cells), 4, axis=2).reshape(cycles, 8 * cells)
        hits = (rows_of[:, None] == own_rows[None, :]).astype(F32)
        return jnp.dot(hits.T, spread, precision=lax.Precision.HIGHEST)

    next_rows = arrived[:, 2 * cells].astype(jnp.int32)
    kick = kick_of(by_axis, gas_map) + kick_of(arrived[:, : 2 * cells], next_rows)
    kick = kick.reshape(gas_cycles, 2, 4 * cells)
    gas_out = gas_velocity - kick / gas_density[:, None, :]
    return (coag_density, velocity_out, gas_out)


def solution(mesh):
    placed = (
        P("rad", "az", None),
        P("rad", "az", None, None),
        P("rad", "az"),
        P("rad", None, "az"),
        P(),
        P(),
        P("rad"),
        P(),
        P("rad"),
    )
    return jax.shard_map(
        body,
        mesh=mesh,
        in_specs=placed,
        out_specs=(P("rad", "az", None), P("rad", "az", None, None), P("rad", None, "az")),
        check_vma=False,
    )
```

```python
import math

import jax
import jax.numpy as jnp
from jax import lax
from jax.sharding import PartitionSpec as P
from jax.experimental import pallas as pl
from jax.experimental.pallas import tpu as pltpu
import functools

F32 = jnp.float32
BF16 = jnp.bfloat16


def split(x):
    hi = x.astype(BF16)
    lo = (x - hi.astype(F32)).astype(BF16)
    return hi, lo


def coag_kernel(n_ref, k_ref, f_ref, o_ref, nt_ref, gain_ref, rhs_ref, *, group):
    bins = k_ref.shape[0]
    nt = n_ref[...].T
    nt_ref[...] = nt
    n_hi, n_lo = split(nt)
    rhs_ref[...] = jnp.concatenate([n_hi, n_lo, n_hi], axis=0)

    def three_pass(table):
        t_hi, t_lo = split(table)
        lhs = jnp.concatenate([t_hi, t_hi, t_lo], axis=1)
        return jnp.dot(lhs, rhs_ref[...], preferred_element_type=F32)

    loss = nt * three_pass(k_ref[...])
    gain_ref[...] = jnp.zeros_like(gain_ref)
    rows = lax.broadcasted_iota(jnp.int32, (bins, bins), 0)

    def step(s, carry):
        first = s * group
        tables = [
            jnp.where(f_ref[pl.ds(first + g, 1), :] == rows, k_ref[pl.ds(first + g, 1), :], 0.0)
            for g in range(group)
        ]
        q = three_pass(jnp.concatenate(tables, axis=0))
        acc = gain_ref[...]
        for g in range(group):
            acc = acc + nt_ref[pl.ds(first + g, 1), :] * q[g * bins : (g + 1) * bins]
        gain_ref[...] = acc
        return carry

    lax.fori_loop(0, bins // group, step, 0)
    o_ref[...] = (nt + gain_ref[...] - loss).T


def coag(dens, kernel, fragment_bins, group=16):
    cells, bins = dens.shape
    full = lambda shape: pl.BlockSpec(shape, lambda c: (0, 0))
    return pl.pallas_call(
        functools.partial(coag_kernel, group=group),
        grid=(1,),
        in_specs=[full((cells, bins)), full((bins, bins)), full((bins, bins))],
        out_specs=full((cells, bins)),
        out_shape=jax.ShapeDtypeStruct((cells, bins), F32),
        scratch_shapes=[
            pltpu.VMEM((bins, cells), F32),
            pltpu.VMEM((bins, cells), F32),
            pltpu.VMEM((3 * bins, cells), BF16),
        ],
        cost_estimate=pl.CostEstimate(
            flops=6 * cells * bins**3, transcendentals=0, bytes_accessed=8 * cells * bins
        ),
    )(dens, kernel, fragment_bins)


def from_behind(block, axis, distance):
    devices = range(lax.axis_size(axis))
    route = [((i - distance) % len(devices), i) for i in devices]
    return lax.ppermute(block, axis, route)


def shifted(block, axis, distance):
    devices = range(lax.axis_size(axis))
    route = [(i - distance, i) for i in devices if i - distance in devices]
    return lax.ppermute(block, axis, route)


def sent(block):
    return lax.all_to_all(block.reshape(-1, block.shape[-1]), "az", 0, 0, tiled=True)


def arranged(flat, cycles, cells, count):
    bins = flat.shape[-1]
    parts = flat.reshape(count, cycles // count, cells, -1, bins)
    return jnp.transpose(parts, (1, 0, 2, 3, 4)).reshape(cycles // count, count * cells, -1, bins)


def body(
    dust_density,
    dust_velocity,
    gas_density,
    gas_velocity,
    kernel,
    grain_param,
    cycle_shifts,
    fragment_bins,
    gas_map,
):
    cycles, cells, bins = dust_density.shape
    gas_cycles = gas_density.shape[0]
    az_count = lax.axis_size("az")
    whole = cells * az_count
    own = cycles // az_count
    turns = lax.dynamic_slice(cycle_shifts, (lax.axis_index("az") * own,), (own,))
    flat_velocity = sent(dust_velocity)
    coag_local = coag(dust_density.reshape(cycles * cells, bins), kernel, fragment_bins)
    coag_local, flat_velocity = lax.optimization_barrier((coag_local, flat_velocity))
    flat_density = sent(coag_local)
    flat_density, flat_velocity = lax.optimization_barrier((flat_density, flat_velocity))
    ring_velocity = arranged(flat_velocity, cycles, cells, az_count)
    ring_density = arranged(flat_density, cycles, cells, az_count)
    rings = jnp.concatenate([ring_density, ring_velocity], axis=2)
    doubled = jnp.concatenate([rings, rings], axis=1)
    rings = jnp.stack(
        [lax.dynamic_slice_in_dim(doubled[c], whole - turns[c], whole, 0) for c in range(own)]
    )
    blocks = rings.reshape(own, az_count, cells, -1, bins)
    state = lax.all_to_all(blocks, "az", 1, 0, tiled=False).reshape(cycles, cells, -1, bins)
    coag_density = state[:, :, 0, :]
    moved_velocity = state[:, :, 1:, :]
    coarse_density = gas_density.reshape(gas_cycles, cells, 4).mean(-1)
    coarse_velocity = (
        gas_velocity.reshape(gas_cycles, 2, cells, 4).mean(-1).reshape(gas_cycles, 2 * cells)
    )
    prev_density, prev_velocity = shifted((coarse_density, coarse_velocity), "rad", 1)
    near_density = jnp.concatenate([prev_density, coarse_density], axis=0)
    near_velocity = jnp.concatenate([prev_velocity, coarse_velocity], axis=0)
    first_row = (lax.axis_index("rad") - 1) * gas_cycles
    near_rows = first_row + jnp.arange(2 * gas_cycles, dtype=jnp.int32)
    select = (gas_map[:, None] == near_rows[None, :]).astype(jnp.float32)
    rho_dust = jnp.dot(select, near_density, precision=lax.Precision.HIGHEST)
    u_flat = jnp.dot(select, near_velocity, precision=lax.Precision.HIGHEST)
    u_dust = jnp.transpose(u_flat.reshape(cycles, 2, cells), (0, 2, 1))
    frac = 1.0 - jnp.exp(-rho_dust[:, :, None] / grain_param[None, None, :])
    velocity_out = moved_velocity + (u_dust[:, :, :, None] - moved_velocity) * frac[:, :, None, :]
    momentum = jnp.sum(coag_density[:, :, None, :] * (velocity_out - moved_velocity), axis=3) / bins
    by_axis = jnp.transpose(momentum, (0, 2, 1)).reshape(cycles, 2 * cells)
    message = jnp.concatenate([by_axis, gas_map.astype(F32)[:, None]], axis=1)
    arrived = shifted(message, "rad", -1)
    own_rows = near_rows[gas_cycles:]

    def kick_of(values, rows_of):
        spread = jnp.repeat(values.reshape(cycles, 2, cells), 4, axis=2).reshape(cycles, 8 * cells)
        hits = (rows_of[:, None] == own_rows[None, :]).astype(F32)
        return jnp.dot(hits.T, spread, precision=lax.Precision.HIGHEST)

    next_rows = arrived[:, 2 * cells].astype(jnp.int32)
    kick = kick_of(by_axis, gas_map) + kick_of(arrived[:, : 2 * cells], next_rows)
    kick = kick.reshape(gas_cycles, 2, 4 * cells)
    gas_out = gas_velocity - kick / gas_density[:, None, :]
    return (coag_density, velocity_out, gas_out)


def solution(mesh):
    placed = (
        P("rad", "az", None),
        P("rad", "az", None, None),
        P("rad", "az"),
        P("rad", None, "az"),
        P(),
        P(),
        P("rad"),
        P(),
        P("rad"),
    )
    return jax.shard_map(
        body,
        mesh=mesh,
        in_specs=placed,
        out_specs=(P("rad", "az", None), P("rad", "az", None, None), P("rad", None, "az")),
        check_vma=False,
    )
```

```python
import math

import jax
import jax.numpy as jnp
from jax import lax
from jax.sharding import PartitionSpec as P
from jax.experimental import pallas as pl
from jax.experimental.pallas import tpu as pltpu
import functools

F32 = jnp.float32
BF16 = jnp.bfloat16


def split(x):
    hi = x.astype(BF16)
    lo = (x - hi.astype(F32)).astype(BF16)
    return hi, lo


def coag_kernel(n_ref, k_ref, f_ref, o_ref, nt_ref, gain_ref, rhs_ref, *, group):
    bins = k_ref.shape[0]
    nt = n_ref[...].T
    nt_ref[...] = nt
    n_hi, n_lo = split(nt)
    rhs_ref[...] = jnp.concatenate([n_hi, n_lo, n_hi], axis=0)

    def three_pass(table):
        t_hi, t_lo = split(table)
        lhs = jnp.concatenate([t_hi, t_hi, t_lo], axis=1)
        return jnp.dot(lhs, rhs_ref[...], preferred_element_type=F32)

    loss = nt * three_pass(k_ref[...])
    gain_ref[...] = jnp.zeros_like(gain_ref)
    rows = lax.broadcasted_iota(jnp.int32, (bins, bins), 0)

    def step(s, carry):
        first = s * group
        tables = [
            jnp.where(f_ref[pl.ds(first + g, 1), :] == rows, k_ref[pl.ds(first + g, 1), :], 0.0)
            for g in range(group)
        ]
        q = three_pass(jnp.concatenate(tables, axis=0))
        acc = gain_ref[...]
        for g in range(group):
            acc = acc + nt_ref[pl.ds(first + g, 1), :] * q[g * bins : (g + 1) * bins]
        gain_ref[...] = acc
        return carry

    lax.fori_loop(0, bins // group, step, 0)
    o_ref[...] = (nt + gain_ref[...] - loss).T


def coag(dens, kernel, fragment_bins, group=16):
    cells, bins = dens.shape
    full = lambda shape: pl.BlockSpec(shape, lambda c: (0, 0))
    return pl.pallas_call(
        functools.partial(coag_kernel, group=group),
        grid=(1,),
        in_specs=[full((cells, bins)), full((bins, bins)), full((bins, bins))],
        out_specs=full((cells, bins)),
        out_shape=jax.ShapeDtypeStruct((cells, bins), F32),
        scratch_shapes=[
            pltpu.VMEM((bins, cells), F32),
            pltpu.VMEM((bins, cells), F32),
            pltpu.VMEM((3 * bins, cells), BF16),
        ],
        cost_estimate=pl.CostEstimate(
            flops=6 * cells * bins**3, transcendentals=0, bytes_accessed=8 * cells * bins
        ),
    )(dens, kernel, fragment_bins)


def from_behind(block, axis, distance):
    devices = range(lax.axis_size(axis))
    route = [((i - distance) % len(devices), i) for i in devices]
    return lax.ppermute(block, axis, route)


def shifted(block, axis, distance):
    devices = range(lax.axis_size(axis))
    route = [(i - distance, i) for i in devices if i - distance in devices]
    return lax.ppermute(block, axis, route)


def sent(block):
    return lax.all_to_all(block.reshape(-1, block.shape[-1]), "az", 0, 0, tiled=True)


def arranged(flat, cycles, cells, count):
    bins = flat.shape[-1]
    parts = flat.reshape(count, cycles // count, cells, -1, bins)
    return jnp.transpose(parts, (1, 0, 2, 3, 4)).reshape(cycles // count, count * cells, -1, bins)


def body(
    dust_density,
    dust_velocity,
    gas_density,
    gas_velocity,
    kernel,
    grain_param,
    cycle_shifts,
    fragment_bins,
    gas_map,
):
    cycles, cells, bins = dust_density.shape
    gas_cycles = gas_density.shape[0]
    az_count = lax.axis_size("az")
    whole = cells * az_count
    own = cycles // az_count
    turns = lax.dynamic_slice(cycle_shifts, (lax.axis_index("az") * own,), (own,))
    flat_velocity = sent(dust_velocity)
    coag_local = coag(dust_density.reshape(cycles * cells, bins), kernel, fragment_bins)
    coag_local, flat_velocity = lax.optimization_barrier((coag_local, flat_velocity))
    flat_density = sent(coag_local)
    flat_density, flat_velocity = lax.optimization_barrier((flat_density, flat_velocity))
    ring_velocity = arranged(flat_velocity, cycles, cells, az_count)
    ring_density = arranged(flat_density, cycles, cells, az_count)
    rings = jnp.concatenate([ring_density, ring_velocity], axis=2)
    doubled = jnp.concatenate([rings, rings], axis=1)
    rings = jnp.stack(
        [lax.dynamic_slice_in_dim(doubled[c], whole - turns[c], whole, 0) for c in range(own)]
    )
    blocks = rings.reshape(own, az_count, cells, -1, bins)
    state = lax.all_to_all(blocks, "az", 1, 0, tiled=False).reshape(cycles, cells, -1, bins)
    coag_density = state[:, :, 0, :]
    moved_velocity = state[:, :, 1:, :]
    coarse_density = gas_density.reshape(gas_cycles, cells, 4).mean(-1)
    coarse_velocity = (
        gas_velocity.reshape(gas_cycles, 2, cells, 4).mean(-1).reshape(gas_cycles, 2 * cells)
    )
    prev_density, prev_velocity = shifted((coarse_density, coarse_velocity), "rad", 1)
    near_density = jnp.concatenate([prev_density, coarse_density], axis=0)
    near_velocity = jnp.concatenate([prev_velocity, coarse_velocity], axis=0)
    first_row = (lax.axis_index("rad") - 1) * gas_cycles
    near_rows = first_row + jnp.arange(2 * gas_cycles, dtype=jnp.int32)
    select = (gas_map[:, None] == near_rows[None, :]).astype(jnp.float32)
    rho_dust = jnp.dot(select, near_density, precision=lax.Precision.HIGHEST)
    u_flat = jnp.dot(select, near_velocity, precision=lax.Precision.HIGHEST)
    u_dust = jnp.transpose(u_flat.reshape(cycles, 2, cells), (0, 2, 1))
    frac = 1.0 - jnp.exp(-rho_dust[:, :, None] / grain_param[None, None, :])
    velocity_out = moved_velocity + (u_dust[:, :, :, None] - moved_velocity) * frac[:, :, None, :]
    momentum = jnp.sum(coag_density[:, :, None, :] * (velocity_out - moved_velocity), axis=3) / bins
    by_axis = jnp.transpose(momentum, (0, 2, 1)).reshape(cycles, 2 * cells)
    message = jnp.concatenate([by_axis, gas_map.astype(F32)[:, None]], axis=1)
    message, moved_velocity, u_dust, frac = lax.optimization_barrier(
        (message, moved_velocity, u_dust, frac)
    )
    velocity_out = moved_velocity + (u_dust[:, :, :, None] - moved_velocity) * frac[:, :, None, :]
    arrived = shifted(message, "rad", -1)
    own_rows = near_rows[gas_cycles:]

    def kick_of(values, rows_of):
        spread = jnp.repeat(values.reshape(cycles, 2, cells), 4, axis=2).reshape(cycles, 8 * cells)
        hits = (rows_of[:, None] == own_rows[None, :]).astype(F32)
        return jnp.dot(hits.T, spread, precision=lax.Precision.HIGHEST)

    next_rows = arrived[:, 2 * cells].astype(jnp.int32)
    kick = kick_of(by_axis, gas_map) + kick_of(arrived[:, : 2 * cells], next_rows)
    kick = kick.reshape(gas_cycles, 2, 4 * cells)
    gas_out = gas_velocity - kick / gas_density[:, None, :]
    return (coag_density, velocity_out, gas_out)


def solution(mesh):
    placed = (
        P("rad", "az", None),
        P("rad", "az", None, None),
        P("rad", "az"),
        P("rad", None, "az"),
        P(),
        P(),
        P("rad"),
        P(),
        P("rad"),
    )
    return jax.shard_map(
        body,
        mesh=mesh,
        in_specs=placed,
        out_specs=(P("rad", "az", None), P("rad", "az", None, None), P("rad", None, "az")),
        check_vma=False,
    )
```

```python
import math

import jax
import jax.numpy as jnp
from jax import lax
from jax.sharding import PartitionSpec as P
from jax.experimental import pallas as pl
from jax.experimental.pallas import tpu as pltpu
import functools

F32 = jnp.float32
BF16 = jnp.bfloat16


def split(x):
    hi = x.astype(BF16)
    lo = (x - hi.astype(F32)).astype(BF16)
    return hi, lo


def coag_kernel(n_ref, k_ref, f_ref, o_ref, nt_ref, gain_ref, rhs_ref, *, group):
    bins = k_ref.shape[0]
    nt = n_ref[...].T
    nt_ref[...] = nt
    n_hi, n_lo = split(nt)
    rhs_ref[...] = jnp.concatenate([n_hi, n_lo, n_hi], axis=0)

    def three_pass(table):
        t_hi, t_lo = split(table)
        lhs = jnp.concatenate([t_hi, t_hi, t_lo], axis=1)
        return jnp.dot(lhs, rhs_ref[...], preferred_element_type=F32)

    loss = nt * three_pass(k_ref[...])
    gain_ref[...] = jnp.zeros_like(gain_ref)
    rows = lax.broadcasted_iota(jnp.int32, (bins, bins), 0)

    def step(s, carry):
        first = s * group
        tables = [
            jnp.where(f_ref[pl.ds(first + g, 1), :] == rows, k_ref[pl.ds(first + g, 1), :], 0.0)
            for g in range(group)
        ]
        q = three_pass(jnp.concatenate(tables, axis=0))
        acc = gain_ref[...]
        for g in range(group):
            acc = acc + nt_ref[pl.ds(first + g, 1), :] * q[g * bins : (g + 1) * bins]
        gain_ref[...] = acc
        return carry

    lax.fori_loop(0, bins // group, step, 0)
    o_ref[...] = (nt + gain_ref[...] - loss).T


def coag(dens, kernel, fragment_bins, group=16):
    cells, bins = dens.shape
    full = lambda shape: pl.BlockSpec(shape, lambda c: (0, 0))
    return pl.pallas_call(
        functools.partial(coag_kernel, group=group),
        grid=(1,),
        in_specs=[full((cells, bins)), full((bins, bins)), full((bins, bins))],
        out_specs=full((cells, bins)),
        out_shape=jax.ShapeDtypeStruct((cells, bins), F32),
        scratch_shapes=[
            pltpu.VMEM((bins, cells), F32),
            pltpu.VMEM((bins, cells), F32),
            pltpu.VMEM((3 * bins, cells), BF16),
        ],
        cost_estimate=pl.CostEstimate(
            flops=6 * cells * bins**3, transcendentals=0, bytes_accessed=8 * cells * bins
        ),
    )(dens, kernel, fragment_bins)


def from_behind(block, axis, distance):
    devices = range(lax.axis_size(axis))
    route = [((i - distance) % len(devices), i) for i in devices]
    return lax.ppermute(block, axis, route)


def shifted(block, axis, distance):
    devices = range(lax.axis_size(axis))
    route = [(i - distance, i) for i in devices if i - distance in devices]
    return lax.ppermute(block, axis, route)


def sent(block):
    return lax.all_to_all(block.reshape(-1, block.shape[-1]), "az", 0, 0, tiled=True)


def arranged(flat, cycles, cells, count):
    bins = flat.shape[-1]
    parts = flat.reshape(count, cycles // count, cells, -1, bins)
    return jnp.transpose(parts, (1, 0, 2, 3, 4)).reshape(cycles // count, count * cells, -1, bins)


def body(
    dust_density,
    dust_velocity,
    gas_density,
    gas_velocity,
    kernel,
    grain_param,
    cycle_shifts,
    fragment_bins,
    gas_map,
):
    cycles, cells, bins = dust_density.shape
    gas_cycles = gas_density.shape[0]
    az_count = lax.axis_size("az")
    whole = cells * az_count
    own = cycles // az_count
    turns = lax.dynamic_slice(cycle_shifts, (lax.axis_index("az") * own,), (own,))
    flat_velocity = sent(dust_velocity)
    coag_local = coag(dust_density.reshape(cycles * cells, bins), kernel, fragment_bins)
    coag_local, flat_velocity = lax.optimization_barrier((coag_local, flat_velocity))
    flat_density = sent(coag_local)
    flat_density, flat_velocity = lax.optimization_barrier((flat_density, flat_velocity))
    ring_velocity = arranged(flat_velocity, cycles, cells, az_count)
    ring_density = arranged(flat_density, cycles, cells, az_count)
    rings = jnp.concatenate([ring_density, ring_velocity], axis=2)
    doubled = jnp.concatenate([rings, rings], axis=1)
    rings = jnp.stack(
        [lax.dynamic_slice_in_dim(doubled[c], whole - turns[c], whole, 0) for c in range(own)]
    )
    blocks = rings.reshape(own, az_count, cells, -1, bins)
    state = lax.all_to_all(blocks, "az", 1, 0, tiled=False).reshape(cycles, cells, -1, bins)
    coag_density = state[:, :, 0, :]
    moved_velocity = state[:, :, 1:, :]
    coarse_density = gas_density.reshape(gas_cycles, cells, 4).mean(-1)
    coarse_velocity = (
        gas_velocity.reshape(gas_cycles, 2, cells, 4).mean(-1).reshape(gas_cycles, 2 * cells)
    )
    prev_density, prev_velocity = shifted((coarse_density, coarse_velocity), "rad", 1)
    near_density = jnp.concatenate([prev_density, coarse_density], axis=0)
    near_velocity = jnp.concatenate([prev_velocity, coarse_velocity], axis=0)
    first_row = (lax.axis_index("rad") - 1) * gas_cycles
    near_rows = first_row + jnp.arange(2 * gas_cycles, dtype=jnp.int32)
    select = (gas_map[:, None] == near_rows[None, :]).astype(jnp.float32)
    rho_dust = jnp.dot(select, near_density, precision=lax.Precision.HIGHEST)
    u_flat = jnp.dot(select, near_velocity, precision=lax.Precision.HIGHEST)
    u_dust = jnp.transpose(u_flat.reshape(cycles, 2, cells), (0, 2, 1))
    frac = 1.0 - jnp.exp(-rho_dust[:, :, None] / grain_param[None, None, :])
    velocity_out = moved_velocity + (u_dust[:, :, :, None] - moved_velocity) * frac[:, :, None, :]
    momentum = jnp.sum(coag_density[:, :, None, :] * (velocity_out - moved_velocity), axis=3) / bins
    by_axis = jnp.transpose(momentum, (0, 2, 1)).reshape(cycles, 2 * cells)
    message = jnp.concatenate([by_axis, gas_map.astype(F32)[:, None]], axis=1)
    message, state, u_dust, frac = lax.optimization_barrier((message, state, u_dust, frac))
    moved_velocity = state[:, :, 1:, :]
    velocity_out = moved_velocity + (u_dust[:, :, :, None] - moved_velocity) * frac[:, :, None, :]
    arrived = shifted(message, "rad", -1)
    own_rows = near_rows[gas_cycles:]

    def kick_of(values, rows_of):
        spread = jnp.repeat(values.reshape(cycles, 2, cells), 4, axis=2).reshape(cycles, 8 * cells)
        hits = (rows_of[:, None] == own_rows[None, :]).astype(F32)
        return jnp.dot(hits.T, spread, precision=lax.Precision.HIGHEST)

    next_rows = arrived[:, 2 * cells].astype(jnp.int32)
    kick = kick_of(by_axis, gas_map) + kick_of(arrived[:, : 2 * cells], next_rows)
    kick = kick.reshape(gas_cycles, 2, 4 * cells)
    gas_out = gas_velocity - kick / gas_density[:, None, :]
    return (coag_density, velocity_out, gas_out)


def solution(mesh):
    placed = (
        P("rad", "az", None),
        P("rad", "az", None, None),
        P("rad", "az"),
        P("rad", None, "az"),
        P(),
        P(),
        P("rad"),
        P(),
        P("rad"),
    )
    return jax.shard_map(
        body,
        mesh=mesh,
        in_specs=placed,
        out_specs=(P("rad", "az", None), P("rad", "az", None, None), P("rad", None, "az")),
        check_vma=False,
    )
```
